256 devices in a mesh: req: 64 (over z, y, core), tp: 4 (over x).
Axes of the slice: x: 4, y: 4, z: 8, core: 2. Of those that a mesh axis runs over, the one named last changes fastest.
Arguments:
- hidden_in: bfloat16 [8192, 2048], P('req'), may hold values from -6 to 6
- attn_gain: float32 [2048], replicated, may hold values from 0.1 to 1.9
- w_query: bfloat16 [2048, 3072], P(None, 'tp'), may hold values from -0.125 to 0.125
- w_latent: bfloat16 [2048, 576], P(None, 'tp'), may hold values from -0.125 to 0.125
- kv_gain: float32 [512], replicated, may hold values from 0.1 to 1.9
- w_key_up: bfloat16 [512, 2048], P(None, 'tp'), may hold values from -0.25 to 0.25
- w_value_up: bfloat16 [512, 2048], P(None, 'tp'), may hold values from -0.25 to 0.25
- w_out: bfloat16 [2048, 2048], P('tp'), may hold values from -0.125 to 0.125
- moe_gain: float32 [2048], replicated, may hold values from 0.1 to 1.9
- w_gate: bfloat16 [64, 2048, 1408], P('req', None, 'tp'), may hold values from -0.125 to 0.125
- w_up: bfloat16 [64, 2048, 1408], P('req', None, 'tp'), may hold values from -0.125 to 0.125
- w_down: bfloat16 [64, 1408, 2048], P('req', 'tp'), may hold values from -0.15625 to 0.15625
- latent_cache: bfloat16 [2048, 64, 576], P('req'), may hold values from -3000 to 3000
- page_table: int32 [256, 8], P('req'), may hold values from 0 to 7, as said below
- cache_len: int32 [256], P('req'), may hold values from 1 to 512, 65536 in all
- parents: int32 [256, 3, 8], P('req'), may hold values from 0 to 7
- routes: int32 [8192, 6], P('req'), may hold values from 0 to 63, all different within a row; in each aligned block of 128 rows (0 to 127, 128 to 255, ...) at most 24 rows name the same one
- route_weights: float32 [8192, 6], P('req'), may hold values from 0.1 to 1
Outputs:
- layer_out: bfloat16 [8192, 2048], P('req', 'tp')
The draws below stay inside these ranges and needn't reach their ends.
Inputs may be any that keep to these rules, and one draw needn't show every extreme that they name: `page_table`: each request's row lists the 8 pages of that request's block of the pool, each once. `routes`: each row names 6 different experts; in the rows of one index of req no expert is named more than 24 times, a bound that some block reaches.
All inputs are finite; a program needn't handle non-finite values. No bound on the sum of `cache_len` on one device may be relied on, other than what follows from the above.
Results may differ from the reference program's by a relative error of at most 0.015.
The reference program's roundings to bfloat16 on the way count: a program that leaves them out, or rounds other values in their place, can miss the bound.
Values may be sent and summed in bfloat16 or wider, within the bound.
No kernel may reach another device: no remote copies, remote signals or barrier semaphores. Data moves between devices by JAX's collectives and lax.ppermute only.
A program may use at most 128 MiB of HBM per device.

```python
import math
import jax
import jax.numpy as jnp
import numpy as np
from jax import lax

D = 2048
HEADS = 16
NOPE = 128
ROPE = 64
VDIM = 128
LATENT = 512
FFE = 1408
TOPK = 6
BEAMS = 8
STEPS = 4
PAGE = 64
PAGES = 8
EXPERTS = 64
MAXLEN = 512
REQS = 256
ROWS_DEV = 128
ROWS = 8192
CAP = 24
N_REQ = 64


def draw_latent_cache(key, part):
    base_key = jax.random.fold_in(jax.random.fold_in(key, 11), 0)
    shape = (REQS * PAGES, PAGE, LATENT + ROPE)
    values = jax.random.normal(base_key, shape, jnp.float32)
    return values.astype(jnp.bfloat16)


def draw_page_table(key, part):
    row_keys = jax.random.split(jax.random.fold_in(key, 23), REQS)
    return jax.vmap(lambda row_key: jax.random.permutation(row_key, PAGES))(row_keys).astype(jnp.int32)


def set_ends(values, stream_key, least, top_value):
    extent = values.shape
    spot = [jax.random.randint(jax.random.fold_in(stream_key, axis), (), 0, extent[axis]) for axis in range(len(extent))]
    values = values.at[tuple(spot)].set(least)
    longest = extent.index(max(extent))
    spot[longest] = (spot[longest] + 1) % extent[longest]
    return values.at[tuple(spot)].set(top_value)


def steps_of(key, extent, cuts, smallest, top_value):
    factor_of = 1.0
    for position, blocks in cuts:
        steps = jax.random.uniform(jax.random.fold_in(jax.random.fold_in(key, 6), position), (blocks,), jnp.float32, smallest / len(cuts), top_value / len(cuts))
        factor_of = factor_of * jnp.repeat(jnp.exp(steps), extent[position] // blocks).reshape((-1,) + (1,) * (len(extent) - 1 - position))
    return factor_of


def split_up(number_of, total, reach, lean):
    portions = [(1 << 20) // math.isqrt(grade ** lean) + 1 for grade in range(2, number_of + 1)]
    surplus, given = total - reach - (number_of - 1), [1] * (number_of - 1)
    while surplus > 0:
        movable = [i for i in range(number_of - 1) if given[i] < reach]
        pool, left = sum([portions[i] for i in movable]), surplus
        for i in movable:
            addition = min(reach - given[i], max(1, left * portions[i] // pool), surplus)
            given[i] = given[i] + addition
            surplus = surplus - addition
    return np.array([reach] + given)


def ragged(key, number_of, total, reach, lean):
    if number_of == 2:
        one = jax.random.randint(key, (), max(1, total - reach), min(reach, total - 1) + 1)
        return jnp.stack([one, total - one])
    sizes = jnp.asarray(split_up(number_of, total, reach, lean), jnp.int32)
    twos = (number_of - 1) // 2
    donor, receiver = sizes[1:1 + 2 * twos:2], sizes[2:2 + 2 * twos:2]
    room = jnp.minimum(donor - 1, reach - receiver)
    shifted = jax.random.randint(jax.random.fold_in(key, 1), (twos,), 0, 1 << 20) % (room + 1)
    sizes = sizes.at[1:1 + 2 * twos:2].set(donor - shifted).at[2:2 + 2 * twos:2].set(receiver + shifted)
    return sizes[jax.random.permutation(jax.random.fold_in(key, 2), number_of)]


def deal_out(stream_key, own, number, rows, number_of, top, limit, slope):
    ranking = jax.random.permutation(stream_key, number_of)
    crowded, ordinary = load_shares(number_of, rows * top, limit, slope, True), load_shares(number_of, rows * top, limit, slope, False)
    places = jnp.arange(number_of)

    def named(sizes, offset_by):
        used = int((sizes > 0).sum())
        fixed = max(1, used // 4)
        passed = fixed + (places - fixed + offset_by * (used - fixed)) % max(1, number_of - fixed)
        return jnp.zeros((number_of,), jnp.int32).at[ranking[jnp.where(places < fixed, places, passed)]].set(jnp.asarray(sizes, jnp.int32))

    sizes = jnp.where(number % 4 == 0, named(crowded, number // 4), named(ordinary, number - number // 4 - 1))
    mixed = jax.random.permutation(jax.random.fold_in(own, 3), number_of)
    donor, taker = mixed[0:number_of // 2 * 2:2], mixed[1:number_of // 2 * 2:2]
    margin = jnp.minimum(sizes[donor] - 1, limit - sizes[taker]) // 2
    margin = jnp.where((donor == ranking[0]) | (taker == ranking[0]) | (sizes[taker] == 0), 0, jnp.maximum(margin, 0))
    passed = jax.random.randint(jax.random.fold_in(own, 4), (number_of // 2,), 0, 1 << 20) % (margin + 1)
    sizes = sizes.at[donor].add(-passed).at[taker].add(passed)
    items = jnp.searchsorted(jnp.cumsum(sizes), jnp.arange(rows * top), side="right").astype(jnp.int32)
    table = items.reshape(top, rows).T
    table = table[jax.random.permutation(jax.random.fold_in(own, 1), rows)]
    offset_by = jax.random.randint(jax.random.fold_in(own, 2), (rows, 1), 0, top)
    return jnp.take_along_axis(table, (jnp.arange(top)[None, :] + offset_by) % top, axis=1)


def load_shares(count, total, reach, slope, full):
    portions = [(1 << 20) // math.isqrt(grade ** slope) + 1 for grade in range(1, count + 1)]
    largest = reach if full else min(reach, max(-(-total // count), total * portions[0] // sum(portions)))
    least = 1 if total - largest >= count - 1 else 0
    given, rest = [largest] + [least] * (count - 1), total - largest - least * (count - 1)
    while rest > 0:
        free = [i for i in range(1, count) if given[i] < largest] or [i for i in range(1, count) if given[i] < reach]
        whole, left = sum([portions[i] for i in free]), rest
        for i in free:
            more = min(reach - given[i], max(1, left * portions[i] // whole), rest)
            given[i] = given[i] + more
            rest = rest - more
    return np.array(given)


def gaussian(stream_key, shape, spread, bound, cuts=(), kind=jnp.bfloat16):
    values = spread * jax.random.normal(stream_key, shape, jnp.float32)
    if cuts:
        values = values * steps_of(stream_key, shape, cuts, -0.22, 0.18)
    return jnp.clip(values, -bound, bound).astype(kind)


def setup_inputs(seed: int = 0) -> dict:
    splits = jax.random.split(jax.random.key(seed), 19)
    hidden_in = gaussian(splits[0], (ROWS, D), 1.0, 6.0, ((0, 64),))
    attn_gain = jnp.clip(1.0 + 0.18 * jax.random.normal(splits[1], (D,), jnp.float32), 0.1, 1.9)
    w_query = gaussian(splits[2], (D, HEADS * (NOPE + ROPE)), D ** -0.5, 0.125, ((1, 4),))
    w_latent = gaussian(splits[3], (D, LATENT + ROPE), D ** -0.5, 0.125, ((1, 4),))
    kv_gain = jnp.clip(1.0 + 0.18 * jax.random.normal(splits[4], (LATENT,), jnp.float32), 0.1, 1.9)
    w_key_up = gaussian(splits[5], (LATENT, HEADS * NOPE), LATENT ** -0.5, 0.25, ((1, 4),))
    w_value_up = gaussian(splits[6], (LATENT, HEADS * VDIM), LATENT ** -0.5, 0.25, ((1, 4),))
    w_out = gaussian(splits[7], (HEADS * VDIM, D), (HEADS * VDIM) ** -0.5, 0.125, ((0, 4),))
    moe_gain = jnp.clip(1.0 + 0.18 * jax.random.normal(splits[8], (D,), jnp.float32), 0.1, 1.9)
    w_gate = gaussian(splits[9], (EXPERTS, D, FFE), D ** -0.5, 0.125, ((0, 64), (2, 4)))
    w_up = gaussian(splits[10], (EXPERTS, D, FFE), D ** -0.5, 0.125, ((0, 64), (2, 4)))
    w_down = gaussian(splits[11], (EXPERTS, FFE, D), FFE ** -0.5, 0.15625, ((0, 64), (1, 4)))
    latent_cache = draw_latent_cache(jax.random.fold_in(splits[18], 71), 0)
    page_table = draw_page_table(jax.random.fold_in(splits[18], 71), 0)
    cache_len = ragged(splits[14], REQS, REQS * MAXLEN // 2, MAXLEN, 2).astype(jnp.int32)
    parents = set_ends(jax.random.randint(splits[15], (REQS, STEPS - 1, BEAMS), 0, BEAMS), jax.random.fold_in(splits[15], 1), 0, BEAMS - 1).astype(jnp.int32)
    routes_keys = jax.random.split(jax.random.fold_in(splits[16], 1), ROWS // ROWS_DEV)
    routes_turns = jax.random.permutation(jax.random.fold_in(splits[16], 3), ROWS // ROWS_DEV)
    routes = jax.vmap(lambda own, number: deal_out(jax.random.fold_in(splits[16], 2), own, number, ROWS_DEV, EXPERTS, TOPK, CAP, 2))(routes_keys, routes_turns).reshape((ROWS, TOPK))
    route_weights = jnp.clip(jnp.exp(math.log(1.0) - 2.3025851 * jax.random.uniform(splits[17], (ROWS, TOPK), jnp.float32) ** steps_of(splits[17], (ROWS, TOPK), ((0, 64),), -0.2, 0.2)), 0.1, 1.0)
    return {"hidden_in": hidden_in, "attn_gain": attn_gain, "w_query": w_query, "w_latent": w_latent, "kv_gain": kv_gain, "w_key_up": w_key_up, "w_value_up": w_value_up, "w_out": w_out, "moe_gain": moe_gain, "w_gate": w_gate, "w_up": w_up, "w_down": w_down, "latent_cache": latent_cache, "page_table": page_table, "cache_len": cache_len, "parents": parents, "routes": routes, "route_weights": route_weights}


eps = 1e-06
rope_base = 50000.0

def rms_scale(values):
    return lax.rsqrt(lax.optimization_barrier(jnp.mean(values * values, axis=-1, keepdims=True)) + eps)

def rotate(values, cos_val, sin_val):
    half_rope = values.shape[-1] // 2
    first = values[..., :half_rope]
    second = values[..., half_rope:]
    return jnp.concatenate([first * cos_val - second * sin_val, second * cos_val + first * sin_val], axis=-1)

def held(values):
    return lax.optimization_barrier(values.astype(jnp.bfloat16)).astype(jnp.float32)

def reference(hidden_in, attn_gain, w_query, w_latent, kv_gain, w_key_up, w_value_up, w_out, moe_gain, w_gate, w_up, w_down, latent_cache, page_table, cache_len, parents, routes, route_weights):
    highest = lax.Precision.HIGHEST
    hidden_f = hidden_in.astype(jnp.float32)
    normed = (hidden_f * rms_scale(hidden_f) * attn_gain).astype(jnp.bfloat16)
    positions = (cache_len.astype(jnp.float32)[:, None, None] + jnp.arange(STEPS, dtype=jnp.float32)[None, :, None] + jnp.zeros((1, 1, BEAMS), jnp.float32)).reshape(ROWS)
    frequency = rope_base ** (-2.0 * jnp.arange(ROPE // 2, dtype=jnp.float32) / ROPE)
    angles = positions[:, None] * frequency[None, :]
    cos_val = jnp.cos(angles)
    sin_val = jnp.sin(angles)
    queries = jnp.dot(normed, w_query, preferred_element_type=jnp.float32).reshape(ROWS, HEADS, NOPE + ROPE)
    q_nope = held(queries[:, :, :NOPE])
    q_rope = held(rotate(queries[:, :, NOPE:], cos_val[:, None, :], sin_val[:, None, :]))
    kv_all = jnp.dot(normed, w_latent, preferred_element_type=jnp.float32)
    new_lat = kv_all[:, :LATENT] * rms_scale(kv_all[:, :LATENT]) * kv_gain
    new_rope = rotate(kv_all[:, LATENT:], cos_val, sin_val)
    new_keys = held(jnp.concatenate([new_lat, new_rope], axis=1))
    key_up = w_key_up.astype(jnp.float32).reshape(LATENT, HEADS, NOPE)
    q_lat = held(jnp.einsum('nhc,lhc->nhl', q_nope, key_up, precision=highest))
    query_key = jnp.concatenate([q_lat, q_rope], axis=2)
    pool_index = (jnp.arange(REQS, dtype=jnp.int32) * PAGES)[:, None] + page_table.astype(jnp.int32)
    cache_keys = jnp.take(latent_cache, pool_index.reshape(-1), axis=0).reshape(REQS, MAXLEN, LATENT + ROPE).astype(jnp.float32)
    live_mask = jnp.arange(MAXLEN, dtype=jnp.int32)[None, :] < cache_len[:, None]
    score_scale = (NOPE + ROPE) ** (-0.5)
    grouped = query_key.reshape(REQS, STEPS * BEAMS * HEADS, LATENT + ROPE)
    s_cache = jnp.einsum('rqd,rld->rql', grouped, cache_keys, precision=highest) * score_scale
    s_cache = jnp.where(live_mask[:, None, :], s_cache, -jnp.inf).reshape(REQS, STEPS, BEAMS, HEADS, MAXLEN)
    fresh = new_keys.reshape(REQS, STEPS, BEAMS, LATENT + ROPE)
    tail_rows = []
    for step_index in range(STEPS):
        lineage = jnp.broadcast_to(jnp.arange(BEAMS, dtype=jnp.int32)[None, :], (REQS, BEAMS))
        pieces = [None] * STEPS
        for earlier in range(step_index, -1, -1):
            pieces[earlier] = jnp.take_along_axis(fresh[:, earlier], lineage[:, :, None], axis=1)
            if earlier > 0:
                lineage = jnp.take_along_axis(parents[:, earlier - 1], lineage, axis=1)
        for later in range(step_index + 1, STEPS):
            pieces[later] = jnp.zeros((REQS, BEAMS, LATENT + ROPE), jnp.float32)
        tail_rows.append(jnp.stack(pieces, axis=2))
    tail_keys = jnp.stack(tail_rows, axis=1)
    queries_tail = query_key.reshape(REQS, STEPS, BEAMS, HEADS, LATENT + ROPE)
    s_tail = jnp.einsum('rsbhd,rsbjd->rsbhj', queries_tail, tail_keys, precision=highest) * score_scale
    causal = jnp.arange(STEPS)[None, :] <= jnp.arange(STEPS)[:, None]
    s_tail = jnp.where(causal[None, :, None, None, :], s_tail, -jnp.inf)
    top_score = jnp.maximum(lax.optimization_barrier(jnp.max(s_cache, axis=-1)), lax.optimization_barrier(jnp.max(s_tail, axis=-1)))
    e_cache = jnp.exp(s_cache - top_score[..., None])
    e_tail = jnp.exp(s_tail - top_score[..., None])
    total = lax.optimization_barrier(jnp.sum(e_cache, axis=-1)) + lax.optimization_barrier(jnp.sum(e_tail, axis=-1))
    p_cache = held(e_cache / total[..., None])
    p_tail = held(e_tail / total[..., None])
    context = jnp.einsum('rsbhl,rld->rsbhd', p_cache, cache_keys[..., :LATENT], precision=highest)
    context = context + jnp.einsum('rsbhj,rsbjd->rsbhd', p_tail, tail_keys[..., :LATENT], precision=highest)
    context = held(context).reshape(ROWS, HEADS, LATENT)
    value_up = w_value_up.astype(jnp.float32).reshape(LATENT, HEADS, VDIM)
    head_out = jnp.einsum('nhl,lhv->nhv', context, value_up, precision=highest).astype(jnp.bfloat16).reshape(ROWS, HEADS * VDIM)
    attn = jnp.dot(head_out, w_out, preferred_element_type=jnp.float32)
    resid = hidden_f + attn
    moe_in = held(resid * rms_scale(resid) * moe_gain)
    buffer_rows = N_REQ * CAP

    def add_expert(expert, acc):
        hit = routes == expert
        marked = jnp.any(hit, axis=1)
        weight = lax.optimization_barrier(jnp.sum(jnp.where(hit, route_weights, 0.0), axis=1))
        place = jnp.cumsum(marked.astype(jnp.int32)) - 1
        target = jnp.where(marked, place, buffer_rows).astype(jnp.int32)
        buffer = jnp.zeros((buffer_rows, D), jnp.float32).at[target].set(moe_in, mode='drop')
        gate_w = lax.dynamic_index_in_dim(w_gate, expert, 0, False).astype(jnp.float32)
        up_w = lax.dynamic_index_in_dim(w_up, expert, 0, False).astype(jnp.float32)
        down_w = lax.dynamic_index_in_dim(w_down, expert, 0, False).astype(jnp.float32)
        gate_val = jnp.dot(buffer, gate_w, precision=highest)
        up_val = jnp.dot(buffer, up_w, precision=highest)
        act = held(jax.nn.silu(gate_val) * up_val)
        expert_out = held(jnp.dot(act, down_w, precision=highest))
        picked = jnp.take(expert_out, jnp.clip(place, 0, buffer_rows - 1).astype(jnp.int32), axis=0)
        return acc + picked * weight[:, None]
    moe = lax.fori_loop(0, EXPERTS, add_expert, jnp.zeros((ROWS, D), jnp.float32))
    return (resid + moe).astype(jnp.bfloat16)
```

```python
import jax
import jax.numpy as jnp
from jax import lax
from jax.sharding import PartitionSpec as P

D = 2048
NOPE = 128
ROPE = 64
VDIM = 128
LATENT = 512
TOPK = 6
EXP_DEV = 1
BEAMS = 8
STEPS = 4
PAGE = 64
PAGES = 8


eps = 1e-06
rope_base = 50000.0


def rms_scale(values):
    return lax.rsqrt(jnp.mean(values * values, axis=-1, keepdims=True) + eps)


def rotate(values, cos_val, sin_val):
    half_rope = values.shape[-1] // 2
    first = values[..., :half_rope]
    second = values[..., half_rope:]
    return jnp.concatenate(
        [first * cos_val - second * sin_val, second * cos_val + first * sin_val], axis=-1
    )


def expert_math(arrived, gate_w, up_w, down_w):
    gate_val = jnp.einsum("nesd,edf->nesf", arrived, gate_w, preferred_element_type=jnp.float32)
    up_val = jnp.einsum("nesd,edf->nesf", arrived, up_w, preferred_element_type=jnp.float32)
    active = (jax.nn.silu(gate_val) * up_val).astype(jnp.bfloat16)
    return jnp.einsum("nesf,efd->nesd", active, down_w, preferred_element_type=jnp.float32)


def send_home(shares):
    return lax.all_to_all(shares, "req", split_axis=0, concat_axis=0, tiled=True)


def local(
    hidden_in,
    attn_gain,
    w_query,
    w_latent,
    kv_gain,
    w_key_up,
    w_value_up,
    w_out,
    moe_gain,
    w_gate,
    w_up,
    w_down,
    latent_cache,
    page_table,
    cache_len,
    parents,
    routes,
    route_weights,
):
    highest = lax.Precision.HIGHEST
    row_count = hidden_in.shape[0]
    req_local = cache_len.shape[0]
    heads_local = w_value_up.shape[1] // VDIM
    tp_count = lax.axis_size("tp")
    req_count = lax.axis_size("req")
    col_share = D // tp_count
    max_len = PAGES * PAGE
    hidden_f = hidden_in.astype(jnp.float32)
    normed = (hidden_f * rms_scale(hidden_f) * attn_gain).astype(jnp.bfloat16)
    positions = (
        cache_len.astype(jnp.float32)[:, None, None]
        + jnp.arange(STEPS, dtype=jnp.float32)[None, :, None]
        + jnp.zeros((1, 1, BEAMS), jnp.float32)
    ).reshape(row_count)
    frequency = rope_base ** (-2.0 * jnp.arange(ROPE // 2, dtype=jnp.float32) / ROPE)
    angles = positions[:, None] * frequency[None, :]
    cos_val = jnp.cos(angles)
    sin_val = jnp.sin(angles)
    queries = jnp.dot(normed, w_query, preferred_element_type=jnp.float32).reshape(
        row_count, heads_local, NOPE + ROPE
    )
    q_nope = queries[:, :, :NOPE].astype(jnp.bfloat16)
    q_rope = rotate(queries[:, :, NOPE:], cos_val[:, None, :], sin_val[:, None, :]).astype(
        jnp.bfloat16
    )
    kv_part = jnp.dot(normed, w_latent, preferred_element_type=jnp.float32)
    kv_all = lax.all_gather(kv_part, "tp", axis=1, tiled=True)
    new_lat = kv_all[:, :LATENT] * rms_scale(kv_all[:, :LATENT]) * kv_gain
    new_rope = rotate(kv_all[:, LATENT:], cos_val, sin_val)
    new_keys = jnp.concatenate([new_lat, new_rope], axis=1).astype(jnp.bfloat16)
    key_up = w_key_up.reshape(LATENT, heads_local, NOPE)
    q_lat = jnp.einsum("nhc,lhc->nhl", q_nope, key_up, preferred_element_type=jnp.float32).astype(
        jnp.bfloat16
    )
    query_key = jnp.concatenate([q_lat, q_rope], axis=2)
    pool_index = (jnp.arange(req_local, dtype=jnp.int32) * PAGES)[:, None] + page_table
    cache_keys = jnp.take(latent_cache, pool_index.reshape(-1), axis=0).reshape(
        req_local, max_len, LATENT + ROPE
    )
    live_mask = jnp.arange(max_len, dtype=jnp.int32)[None, :] < cache_len[:, None]
    score_scale = (NOPE + ROPE) ** (-0.5)
    grouped = query_key.reshape(req_local, STEPS * BEAMS * heads_local, LATENT + ROPE)
    s_cache = (
        jnp.einsum("rqd,rld->rql", grouped, cache_keys, preferred_element_type=jnp.float32)
        * score_scale
    )
    s_cache = jnp.where(live_mask[:, None, :], s_cache, -jnp.inf).reshape(
        req_local, STEPS, BEAMS, heads_local, max_len
    )
    fresh = new_keys.reshape(req_local, STEPS, BEAMS, LATENT + ROPE).astype(jnp.float32)
    parent_hot = (parents[..., None] == jnp.arange(BEAMS, dtype=jnp.int32)).astype(jnp.float32)
    identity = jnp.broadcast_to(jnp.eye(BEAMS, dtype=jnp.float32), (req_local, BEAMS, BEAMS))
    tail_rows = []
    for step_index in range(STEPS):
        lineage = identity
        pieces = [None] * STEPS
        for earlier in range(step_index, -1, -1):
            pieces[earlier] = jnp.einsum(
                "rba,rad->rbd", lineage, fresh[:, earlier], precision=highest
            )
            if earlier > 0:
                lineage = jnp.einsum(
                    "rba,rac->rbc", lineage, parent_hot[:, earlier - 1], precision=highest
                )
        for later in range(step_index + 1, STEPS):
            pieces[later] = jnp.zeros_like(pieces[0])
        tail_rows.append(jnp.stack(pieces, axis=2))
    tail_keys = jnp.stack(tail_rows, axis=1).astype(jnp.bfloat16)
    queries_tail = query_key.reshape(req_local, STEPS, BEAMS, heads_local, LATENT + ROPE)
    s_tail = (
        jnp.einsum(
            "rsbhd,rsbjd->rsbhj", queries_tail, tail_keys, preferred_element_type=jnp.float32
        )
        * score_scale
    )
    causal = jnp.arange(STEPS)[None, :] <= jnp.arange(STEPS)[:, None]
    s_tail = jnp.where(causal[None, :, None, None, :], s_tail, -jnp.inf)
    top_score = jnp.maximum(jnp.max(s_cache, axis=-1), jnp.max(s_tail, axis=-1))
    e_cache = jnp.exp(s_cache - top_score[..., None])
    e_tail = jnp.exp(s_tail - top_score[..., None])
    total = jnp.sum(e_cache, axis=-1) + jnp.sum(e_tail, axis=-1)
    p_cache = (e_cache / total[..., None]).astype(jnp.bfloat16)
    p_tail = (e_tail / total[..., None]).astype(jnp.bfloat16)
    context = jnp.einsum(
        "rsbhl,rld->rsbhd", p_cache, cache_keys[..., :LATENT], preferred_element_type=jnp.float32
    )
    context = context + jnp.einsum(
        "rsbhj,rsbjd->rsbhd", p_tail, tail_keys[..., :LATENT], preferred_element_type=jnp.float32
    )
    context = context.astype(jnp.bfloat16).reshape(row_count, heads_local, LATENT)
    value_up = w_value_up.reshape(LATENT, heads_local, VDIM)
    head_out = (
        jnp.einsum("nhl,lhv->nhv", context, value_up, preferred_element_type=jnp.float32)
        .astype(jnp.bfloat16)
        .reshape(row_count, heads_local * VDIM)
    )
    attn_part = jnp.dot(head_out, w_out, preferred_element_type=jnp.float32)
    expert_count = EXP_DEV * req_count
    capacity = min(row_count, 2 * row_count * TOPK // expert_count)
    slot_count = expert_count * capacity
    picks = routes.reshape(-1)
    pick_hot = (picks[:, None] == jnp.arange(expert_count, dtype=jnp.int32)[None, :]).astype(
        jnp.int32
    )
    before = jnp.cumsum(pick_hot, axis=0) - pick_hot
    ranks = jnp.sum(before * pick_hot, axis=1)
    slot_of = picks * capacity + ranks
    slot_hot = (slot_of[:, None] == jnp.arange(slot_count, dtype=jnp.int32)[None, :]).reshape(
        row_count, TOPK, slot_count
    )
    gather_rows = jnp.sum(slot_hot.astype(jnp.int32), axis=1).astype(jnp.bfloat16)
    weight_rows = jnp.sum(jnp.where(slot_hot, route_weights[:, :, None], 0.0), axis=1)
    tp_index = lax.axis_index("tp")
    col_start = tp_index * col_share
    attn_cols = lax.psum_scatter(attn_part, "tp", scatter_dimension=1, tiled=True)
    hidden_cols = lax.dynamic_slice_in_dim(hidden_f, col_start, col_share, 1)
    resid_cols = hidden_cols + attn_cols
    square_sum = lax.psum(jnp.sum(resid_cols * resid_cols, axis=-1, keepdims=True), "tp")
    moe_scale = lax.rsqrt(square_sum / D + eps)
    gain_cols = lax.dynamic_slice_in_dim(moe_gain, col_start, col_share, 0)
    moe_in_cols = (resid_cols * moe_scale * gain_cols).astype(jnp.bfloat16)
    placed = jnp.dot(gather_rows.T, moe_in_cols, preferred_element_type=jnp.float32).astype(
        jnp.bfloat16
    )
    arrived_cols = lax.all_to_all(
        placed.reshape(req_count, EXP_DEV, capacity, col_share),
        "req",
        split_axis=0,
        concat_axis=0,
        tiled=True,
    )
    arrived = lax.all_gather(arrived_cols, "tp", axis=3, tiled=True)
    partial_out = expert_math(arrived, w_gate, w_up, w_down)
    shares = lax.psum_scatter(partial_out, "tp", scatter_dimension=3, tiled=True)
    returned = send_home(shares.astype(jnp.bfloat16))
    combined = jnp.dot(
        weight_rows, returned.reshape(slot_count, col_share).astype(jnp.float32), precision=highest
    )
    return (resid_cols + combined).astype(jnp.bfloat16)


def solution(mesh):
    in_specs = (
        P("req", None),
        P(),
        P(None, "tp"),
        P(None, "tp"),
        P(),
        P(None, "tp"),
        P(None, "tp"),
        P("tp", None),
        P(),
        P("req", None, "tp"),
        P("req", None, "tp"),
        P("req", "tp", None),
        P("req", None, None),
        P("req", None),
        P("req"),
        P("req", None, None),
        P("req", None),
        P("req", None),
    )
    out_specs = P("req", "tp")
    return jax.shard_map(local, mesh=mesh, in_specs=in_specs, out_specs=out_specs, check_vma=False)
```

```python
import jax
import jax.numpy as jnp
from jax import lax
from jax.sharding import PartitionSpec as P

D = 2048
NOPE = 128
ROPE = 64
VDIM = 128
LATENT = 512
TOPK = 6
EXP_DEV = 1
BEAMS = 8
STEPS = 4
PAGE = 64
PAGES = 8


eps = 1e-06
rope_base = 50000.0


def rms_scale(values):
    return lax.rsqrt(jnp.mean(values * values, axis=-1, keepdims=True) + eps)


def rotate(values, cos_val, sin_val):
    half_rope = values.shape[-1] // 2
    first = values[..., :half_rope]
    second = values[..., half_rope:]
    return jnp.concatenate(
        [first * cos_val - second * sin_val, second * cos_val + first * sin_val], axis=-1
    )


def expert_math(arrived, gate_w, up_w, down_w):
    gate_val = jnp.einsum("nesd,edf->nesf", arrived, gate_w, preferred_element_type=jnp.float32)
    up_val = jnp.einsum("nesd,edf->nesf", arrived, up_w, preferred_element_type=jnp.float32)
    active = (jax.nn.silu(gate_val) * up_val).astype(jnp.bfloat16)
    return jnp.einsum("nesf,efd->nesd", active, down_w, preferred_element_type=jnp.float32)


def send_home(shares):
    return lax.all_to_all(shares, "req", split_axis=0, concat_axis=0, tiled=True)


def local(
    hidden_in,
    attn_gain,
    w_query,
    w_latent,
    kv_gain,
    w_key_up,
    w_value_up,
    w_out,
    moe_gain,
    w_gate,
    w_up,
    w_down,
    latent_cache,
    page_table,
    cache_len,
    parents,
    routes,
    route_weights,
):
    highest = lax.Precision.HIGHEST
    row_count = hidden_in.shape[0]
    req_local = cache_len.shape[0]
    heads_local = w_value_up.shape[1] // VDIM
    tp_count = lax.axis_size("tp")
    req_count = lax.axis_size("req")
    col_share = D // tp_count
    max_len = PAGES * PAGE
    hidden_f = hidden_in.astype(jnp.float32)
    normed = (hidden_f * rms_scale(hidden_f) * attn_gain).astype(jnp.bfloat16)
    positions = (
        cache_len.astype(jnp.float32)[:, None, None]
        + jnp.arange(STEPS, dtype=jnp.float32)[None, :, None]
        + jnp.zeros((1, 1, BEAMS), jnp.float32)
    ).reshape(row_count)
    frequency = rope_base ** (-2.0 * jnp.arange(ROPE // 2, dtype=jnp.float32) / ROPE)
    angles = positions[:, None] * frequency[None, :]
    cos_val = jnp.cos(angles)
    sin_val = jnp.sin(angles)
    queries = jnp.dot(normed, w_query, preferred_element_type=jnp.float32).reshape(
        row_count, heads_local, NOPE + ROPE
    )
    q_nope = queries[:, :, :NOPE].astype(jnp.bfloat16)
    q_rope = rotate(queries[:, :, NOPE:], cos_val[:, None, :], sin_val[:, None, :]).astype(
        jnp.bfloat16
    )
    kv_part = jnp.dot(normed, w_latent, preferred_element_type=jnp.float32)
    kv_all = lax.all_gather(kv_part, "tp", axis=1, tiled=True)
    new_lat = kv_all[:, :LATENT] * rms_scale(kv_all[:, :LATENT]) * kv_gain
    new_rope = rotate(kv_all[:, LATENT:], cos_val, sin_val)
    new_keys = jnp.concatenate([new_lat, new_rope], axis=1).astype(jnp.bfloat16)
    key_up = w_key_up.reshape(LATENT, heads_local, NOPE)
    q_lat = jnp.einsum("nhc,lhc->nhl", q_nope, key_up, preferred_element_type=jnp.float32).astype(
        jnp.bfloat16
    )
    query_key = jnp.concatenate([q_lat, q_rope], axis=2)
    pool_index = (jnp.arange(req_local, dtype=jnp.int32) * PAGES)[:, None] + page_table
    cache_keys = jnp.take(latent_cache, pool_index.reshape(-1), axis=0).reshape(
        req_local, max_len, LATENT + ROPE
    )
    live_mask = jnp.arange(max_len, dtype=jnp.int32)[None, :] < cache_len[:, None]
    score_scale = (NOPE + ROPE) ** (-0.5)
    grouped = query_key.reshape(req_local, STEPS * BEAMS * heads_local, LATENT + ROPE)
    s_cache = (
        jnp.einsum("rqd,rld->rql", grouped, cache_keys, preferred_element_type=jnp.float32)
        * score_scale
    )
    s_cache = jnp.where(live_mask[:, None, :], s_cache, -jnp.inf).reshape(
        req_local, STEPS, BEAMS, heads_local, max_len
    )
    fresh = new_keys.reshape(req_local, STEPS, BEAMS, LATENT + ROPE).astype(jnp.float32)
    parent_hot = (parents[..., None] == jnp.arange(BEAMS, dtype=jnp.int32)).astype(jnp.float32)
    identity = jnp.broadcast_to(jnp.eye(BEAMS, dtype=jnp.float32), (req_local, BEAMS, BEAMS))
    tail_rows = []
    for step_index in range(STEPS):
        lineage = identity
        pieces = [None] * STEPS
        for earlier in range(step_index, -1, -1):
            pieces[earlier] = jnp.einsum(
                "rba,rad->rbd", lineage, fresh[:, earlier], precision=highest
            )
            if earlier > 0:
                lineage = jnp.einsum(
                    "rba,rac->rbc", lineage, parent_hot[:, earlier - 1], precision=highest
                )
        for later in range(step_index + 1, STEPS):
            pieces[later] = jnp.zeros_like(pieces[0])
        tail_rows.append(jnp.stack(pieces, axis=2))
    tail_keys = jnp.stack(tail_rows, axis=1).astype(jnp.bfloat16)
    queries_tail = query_key.reshape(req_local, STEPS, BEAMS, heads_local, LATENT + ROPE)
    s_tail = (
        jnp.einsum(
            "rsbhd,rsbjd->rsbhj", queries_tail, tail_keys, preferred_element_type=jnp.float32
        )
        * score_scale
    )
    causal = jnp.arange(STEPS)[None, :] <= jnp.arange(STEPS)[:, None]
    s_tail = jnp.where(causal[None, :, None, None, :], s_tail, -jnp.inf)
    top_score = jnp.maximum(jnp.max(s_cache, axis=-1), jnp.max(s_tail, axis=-1))
    e_cache = jnp.exp(s_cache - top_score[..., None])
    e_tail = jnp.exp(s_tail - top_score[..., None])
    total = jnp.sum(e_cache, axis=-1) + jnp.sum(e_tail, axis=-1)
    p_cache = (e_cache / total[..., None]).astype(jnp.bfloat16)
    p_tail = (e_tail / total[..., None]).astype(jnp.bfloat16)
    context = jnp.einsum(
        "rsbhl,rld->rsbhd", p_cache, cache_keys[..., :LATENT], preferred_element_type=jnp.float32
    )
    context = context + jnp.einsum(
        "rsbhj,rsbjd->rsbhd", p_tail, tail_keys[..., :LATENT], preferred_element_type=jnp.float32
    )
    context = context.astype(jnp.bfloat16).reshape(row_count, heads_local, LATENT)
    value_up = w_value_up.reshape(LATENT, heads_local, VDIM)
    head_out = (
        jnp.einsum("nhl,lhv->nhv", context, value_up, preferred_element_type=jnp.float32)
        .astype(jnp.bfloat16)
        .reshape(row_count, heads_local * VDIM)
    )
    attn_part = jnp.dot(head_out, w_out, preferred_element_type=jnp.float32)
    expert_count = EXP_DEV * req_count
    capacity = min(row_count, 2 * row_count * TOPK // expert_count)
    slot_count = expert_count * capacity
    picks = routes.reshape(-1)
    pick_hot = (picks[:, None] == jnp.arange(expert_count, dtype=jnp.int32)[None, :]).astype(
        jnp.int32
    )
    before = jnp.cumsum(pick_hot, axis=0) - pick_hot
    ranks = jnp.sum(before * pick_hot, axis=1)
    slot_of = picks * capacity + ranks
    slot_hot = (slot_of[:, None] == jnp.arange(slot_count, dtype=jnp.int32)[None, :]).reshape(
        row_count, TOPK, slot_count
    )
    gather_rows = jnp.sum(slot_hot.astype(jnp.int32), axis=1).astype(jnp.bfloat16)
    weight_rows = jnp.sum(jnp.where(slot_hot, route_weights[:, :, None], 0.0), axis=1)
    tp_index = lax.axis_index("tp")
    col_start = tp_index * col_share
    attn_cols = lax.psum_scatter(attn_part, "tp", scatter_dimension=1, tiled=True)
    hidden_cols = lax.dynamic_slice_in_dim(hidden_f, col_start, col_share, 1)
    resid_cols = hidden_cols + attn_cols
    square_sum = lax.psum(jnp.sum(resid_cols * resid_cols, axis=-1, keepdims=True), "tp")
    moe_scale = lax.rsqrt(square_sum / D + eps)
    gain_cols = lax.dynamic_slice_in_dim(moe_gain, col_start, col_share, 0)
    moe_in_cols = (resid_cols * moe_scale * gain_cols).astype(jnp.bfloat16)
    placed = jnp.dot(gather_rows.T, moe_in_cols, preferred_element_type=jnp.float32).astype(
        jnp.bfloat16
    )
    arrived_cols = lax.all_to_all(
        placed.reshape(req_count, EXP_DEV, capacity, col_share),
        "req",
        split_axis=0,
        concat_axis=0,
        tiled=True,
    )
    arrived = lax.all_gather(arrived_cols, "tp", axis=3, tiled=True)
    partial_out = expert_math(arrived, w_gate, w_up, w_down)
    shares = lax.psum_scatter(
        partial_out.astype(jnp.bfloat16), "tp", scatter_dimension=3, tiled=True
    )
    returned = send_home(shares)
    combined = jnp.dot(
        weight_rows, returned.reshape(slot_count, col_share).astype(jnp.float32), precision=highest
    )
    return (resid_cols + combined).astype(jnp.bfloat16)


def solution(mesh):
    in_specs = (
        P("req", None),
        P(),
        P(None, "tp"),
        P(None, "tp"),
        P(),
        P(None, "tp"),
        P(None, "tp"),
        P("tp", None),
        P(),
        P("req", None, "tp"),
        P("req", None, "tp"),
        P("req", "tp", None),
        P("req", None, None),
        P("req", None),
        P("req"),
        P("req", None, None),
        P("req", None),
        P("req", None),
    )
    out_specs = P("req", "tp")
    return jax.shard_map(local, mesh=mesh, in_specs=in_specs, out_specs=out_specs, check_vma=False)
```

```python
import jax
import jax.numpy as jnp
from jax import lax
from jax.sharding import PartitionSpec as P

D = 2048
NOPE = 128
ROPE = 64
VDIM = 128
LATENT = 512
TOPK = 6
EXP_DEV = 1
BEAMS = 8
STEPS = 4
PAGE = 64
PAGES = 8
MOE_CHUNKS = 4


eps = 1e-06
rope_base = 50000.0


def rms_scale(values):
    return lax.rsqrt(jnp.mean(values * values, axis=-1, keepdims=True) + eps)


def rotate(values, cos_val, sin_val):
    half_rope = values.shape[-1] // 2
    first = values[..., :half_rope]
    second = values[..., half_rope:]
    return jnp.concatenate(
        [first * cos_val - second * sin_val, second * cos_val + first * sin_val], axis=-1
    )


def expert_math(arrived, gate_w, up_w, down_w):
    gate_val = jnp.einsum("nesd,edf->nesf", arrived, gate_w, preferred_element_type=jnp.float32)
    up_val = jnp.einsum("nesd,edf->nesf", arrived, up_w, preferred_element_type=jnp.float32)
    active = (jax.nn.silu(gate_val) * up_val).astype(jnp.bfloat16)
    return jnp.einsum("nesf,efd->nesd", active, down_w, preferred_element_type=jnp.float32)


def send_home(shares):
    return lax.all_to_all(shares, "req", split_axis=0, concat_axis=0, tiled=True)


def local(
    hidden_in,
    attn_gain,
    w_query,
    w_latent,
    kv_gain,
    w_key_up,
    w_value_up,
    w_out,
    moe_gain,
    w_gate,
    w_up,
    w_down,
    latent_cache,
    page_table,
    cache_len,
    parents,
    routes,
    route_weights,
):
    highest = lax.Precision.HIGHEST
    row_count = hidden_in.shape[0]
    req_local = cache_len.shape[0]
    heads_local = w_value_up.shape[1] // VDIM
    tp_count = lax.axis_size("tp")
    req_count = lax.axis_size("req")
    col_share = D // tp_count
    max_len = PAGES * PAGE
    hidden_f = hidden_in.astype(jnp.float32)
    normed = (hidden_f * rms_scale(hidden_f) * attn_gain).astype(jnp.bfloat16)
    positions = (
        cache_len.astype(jnp.float32)[:, None, None]
        + jnp.arange(STEPS, dtype=jnp.float32)[None, :, None]
        + jnp.zeros((1, 1, BEAMS), jnp.float32)
    ).reshape(row_count)
    frequency = rope_base ** (-2.0 * jnp.arange(ROPE // 2, dtype=jnp.float32) / ROPE)
    angles = positions[:, None] * frequency[None, :]
    cos_val = jnp.cos(angles)
    sin_val = jnp.sin(angles)
    queries = jnp.dot(normed, w_query, preferred_element_type=jnp.float32).reshape(
        row_count, heads_local, NOPE + ROPE
    )
    q_nope = queries[:, :, :NOPE].astype(jnp.bfloat16)
    q_rope = rotate(queries[:, :, NOPE:], cos_val[:, None, :], sin_val[:, None, :]).astype(
        jnp.bfloat16
    )
    kv_part = jnp.dot(normed, w_latent, preferred_element_type=jnp.float32)
    kv_all = lax.all_gather(kv_part, "tp", axis=1, tiled=True)
    new_lat = kv_all[:, :LATENT] * rms_scale(kv_all[:, :LATENT]) * kv_gain
    new_rope = rotate(kv_all[:, LATENT:], cos_val, sin_val)
    new_keys = jnp.concatenate([new_lat, new_rope], axis=1).astype(jnp.bfloat16)
    key_up = w_key_up.reshape(LATENT, heads_local, NOPE)
    q_lat = jnp.einsum("nhc,lhc->nhl", q_nope, key_up, preferred_element_type=jnp.float32).astype(
        jnp.bfloat16
    )
    query_key = jnp.concatenate([q_lat, q_rope], axis=2)
    pool_index = (jnp.arange(req_local, dtype=jnp.int32) * PAGES)[:, None] + page_table
    cache_keys = jnp.take(latent_cache, pool_index.reshape(-1), axis=0).reshape(
        req_local, max_len, LATENT + ROPE
    )
    live_mask = jnp.arange(max_len, dtype=jnp.int32)[None, :] < cache_len[:, None]
    score_scale = (NOPE + ROPE) ** (-0.5)
    grouped = query_key.reshape(req_local, STEPS * BEAMS * heads_local, LATENT + ROPE)
    s_cache = (
        jnp.einsum("rqd,rld->rql", grouped, cache_keys, preferred_element_type=jnp.float32)
        * score_scale
    )
    s_cache = jnp.where(live_mask[:, None, :], s_cache, -jnp.inf).reshape(
        req_local, STEPS, BEAMS, heads_local, max_len
    )
    fresh = new_keys.reshape(req_local, STEPS, BEAMS, LATENT + ROPE).astype(jnp.float32)
    parent_hot = (parents[..., None] == jnp.arange(BEAMS, dtype=jnp.int32)).astype(jnp.float32)
    identity = jnp.broadcast_to(jnp.eye(BEAMS, dtype=jnp.float32), (req_local, BEAMS, BEAMS))
    tail_rows = []
    for step_index in range(STEPS):
        lineage = identity
        pieces = [None] * STEPS
        for earlier in range(step_index, -1, -1):
            pieces[earlier] = jnp.einsum(
                "rba,rad->rbd", lineage, fresh[:, earlier], precision=highest
            )
            if earlier > 0:
                lineage = jnp.einsum(
                    "rba,rac->rbc", lineage, parent_hot[:, earlier - 1], precision=highest
                )
        for later in range(step_index + 1, STEPS):
            pieces[later] = jnp.zeros_like(pieces[0])
        tail_rows.append(jnp.stack(pieces, axis=2))
    tail_keys = jnp.stack(tail_rows, axis=1).astype(jnp.bfloat16)
    queries_tail = query_key.reshape(req_local, STEPS, BEAMS, heads_local, LATENT + ROPE)
    s_tail = (
        jnp.einsum(
            "rsbhd,rsbjd->rsbhj", queries_tail, tail_keys, preferred_element_type=jnp.float32
        )
        * score_scale
    )
    causal = jnp.arange(STEPS)[None, :] <= jnp.arange(STEPS)[:, None]
    s_tail = jnp.where(causal[None, :, None, None, :], s_tail, -jnp.inf)
    top_score = jnp.maximum(jnp.max(s_cache, axis=-1), jnp.max(s_tail, axis=-1))
    e_cache = jnp.exp(s_cache - top_score[..., None])
    e_tail = jnp.exp(s_tail - top_score[..., None])
    total = jnp.sum(e_cache, axis=-1) + jnp.sum(e_tail, axis=-1)
    p_cache = (e_cache / total[..., None]).astype(jnp.bfloat16)
    p_tail = (e_tail / total[..., None]).astype(jnp.bfloat16)
    context = jnp.einsum(
        "rsbhl,rld->rsbhd", p_cache, cache_keys[..., :LATENT], preferred_element_type=jnp.float32
    )
    context = context + jnp.einsum(
        "rsbhj,rsbjd->rsbhd", p_tail, tail_keys[..., :LATENT], preferred_element_type=jnp.float32
    )
    context = context.astype(jnp.bfloat16).reshape(row_count, heads_local, LATENT)
    value_up = w_value_up.reshape(LATENT, heads_local, VDIM)
    head_out = (
        jnp.einsum("nhl,lhv->nhv", context, value_up, preferred_element_type=jnp.float32)
        .astype(jnp.bfloat16)
        .reshape(row_count, heads_local * VDIM)
    )
    attn_part = jnp.dot(head_out, w_out, preferred_element_type=jnp.float32)
    expert_count = EXP_DEV * req_count
    capacity = min(row_count, 2 * row_count * TOPK // expert_count)
    slot_count = expert_count * capacity
    picks = routes.reshape(-1)
    pick_hot = (picks[:, None] == jnp.arange(expert_count, dtype=jnp.int32)[None, :]).astype(
        jnp.int32
    )
    before = jnp.cumsum(pick_hot, axis=0) - pick_hot
    ranks = jnp.sum(before * pick_hot, axis=1)
    slot_of = picks * capacity + ranks
    slot_hot = (slot_of[:, None] == jnp.arange(slot_count, dtype=jnp.int32)[None, :]).reshape(
        row_count, TOPK, slot_count
    )
    gather_rows = jnp.sum(slot_hot.astype(jnp.int32), axis=1).astype(jnp.bfloat16)
    weight_rows = jnp.sum(jnp.where(slot_hot, route_weights[:, :, None], 0.0), axis=1)
    tp_index = lax.axis_index("tp")
    col_start = tp_index * col_share
    attn_cols = lax.psum_scatter(attn_part, "tp", scatter_dimension=1, tiled=True)
    hidden_cols = lax.dynamic_slice_in_dim(hidden_f, col_start, col_share, 1)
    resid_cols = hidden_cols + attn_cols
    square_sum = lax.psum(jnp.sum(resid_cols * resid_cols, axis=-1, keepdims=True), "tp")
    moe_scale = lax.rsqrt(square_sum / D + eps)
    gain_cols = lax.dynamic_slice_in_dim(moe_gain, col_start, col_share, 0)
    moe_in_cols = (resid_cols * moe_scale * gain_cols).astype(jnp.bfloat16)
    placed = jnp.dot(gather_rows.T, moe_in_cols, preferred_element_type=jnp.float32).astype(
        jnp.bfloat16
    )
    placed = placed.reshape(req_count, EXP_DEV, capacity, col_share)
    chunk = capacity // MOE_CHUNKS
    returned_parts = []
    for chunk_index in range(MOE_CHUNKS):
        arrived_cols = lax.all_to_all(
            placed[:, :, chunk_index * chunk : (chunk_index + 1) * chunk],
            "req",
            split_axis=0,
            concat_axis=0,
            tiled=True,
        )
        arrived = lax.all_gather(arrived_cols, "tp", axis=3, tiled=True)
        partial_out = expert_math(arrived, w_gate, w_up, w_down)
        shares = lax.psum_scatter(
            partial_out.astype(jnp.bfloat16), "tp", scatter_dimension=3, tiled=True
        )
        returned_parts.append(send_home(shares))
    returned = jnp.concatenate(returned_parts, axis=2)
    combined = jnp.dot(
        weight_rows, returned.reshape(slot_count, col_share).astype(jnp.float32), precision=highest
    )
    return (resid_cols + combined).astype(jnp.bfloat16)


def solution(mesh):
    in_specs = (
        P("req", None),
        P(),
        P(None, "tp"),
        P(None, "tp"),
        P(),
        P(None, "tp"),
        P(None, "tp"),
        P("tp", None),
        P(),
        P("req", None, "tp"),
        P("req", None, "tp"),
        P("req", "tp", None),
        P("req", None, None),
        P("req", None),
        P("req"),
        P("req", None, None),
        P("req", None),
        P("req", None),
    )
    out_specs = P("req", "tp")
    return jax.shard_map(local, mesh=mesh, in_specs=in_specs, out_specs=out_specs, check_vma=False)
```

```python
import jax
import jax.numpy as jnp
from jax import lax
from jax.sharding import PartitionSpec as P

D = 2048
NOPE = 128
ROPE = 64
VDIM = 128
LATENT = 512
TOPK = 6
EXP_DEV = 1
BEAMS = 8
STEPS = 4
PAGE = 64
PAGES = 8


eps = 1e-06
rope_base = 50000.0


def rms_scale(values):
    return lax.rsqrt(jnp.mean(values * values, axis=-1, keepdims=True) + eps)


def rotate(values, cos_val, sin_val):
    half_rope = values.shape[-1] // 2
    first = values[..., :half_rope]
    second = values[..., half_rope:]
    return jnp.concatenate(
        [first * cos_val - second * sin_val, second * cos_val + first * sin_val], axis=-1
    )


def expert_math(arrived, gate_w, up_w, down_cols):
    gate_val = jnp.einsum("nesd,edf->nesf", arrived, gate_w, preferred_element_type=jnp.float32)
    up_val = jnp.einsum("nesd,edf->nesf", arrived, up_w, preferred_element_type=jnp.float32)
    active = (jax.nn.silu(gate_val) * up_val).astype(jnp.bfloat16)
    active_all = lax.all_gather(active, "tp", axis=3, tiled=True)
    return jnp.einsum(
        "nesf,efd->nesd", active_all, down_cols, preferred_element_type=jnp.float32
    ).astype(jnp.bfloat16)


def down_by_columns(down_w):
    tp_count = lax.axis_size("tp")
    tp_index = lax.axis_index("tp")
    col_share = down_w.shape[2] // tp_count
    pieces = [None] * tp_count
    for shift in range(tp_count):
        target = (tp_index + shift) % tp_count
        piece = lax.dynamic_slice_in_dim(down_w, target * col_share, col_share, 2)
        if shift:
            piece = lax.ppermute(
                piece, "tp", [(s, (s + shift) % tp_count) for s in range(tp_count)]
            )
        pieces[shift] = piece
    stacked = jnp.stack(pieces, axis=0)
    ordered = jnp.take(stacked, (tp_index - jnp.arange(tp_count)) % tp_count, axis=0)
    return jnp.concatenate([ordered[i] for i in range(tp_count)], axis=1)


def send_home(shares):
    return lax.all_to_all(shares, "req", split_axis=0, concat_axis=0, tiled=True)


def local(
    hidden_in,
    attn_gain,
    w_query,
    w_latent,
    kv_gain,
    w_key_up,
    w_value_up,
    w_out,
    moe_gain,
    w_gate,
    w_up,
    w_down,
    latent_cache,
    page_table,
    cache_len,
    parents,
    routes,
    route_weights,
):
    highest = lax.Precision.HIGHEST
    row_count = hidden_in.shape[0]
    req_local = cache_len.shape[0]
    heads_local = w_value_up.shape[1] // VDIM
    tp_count = lax.axis_size("tp")
    req_count = lax.axis_size("req")
    col_share = D // tp_count
    max_len = PAGES * PAGE
    hidden_f = hidden_in.astype(jnp.float32)
    normed = (hidden_f * rms_scale(hidden_f) * attn_gain).astype(jnp.bfloat16)
    positions = (
        cache_len.astype(jnp.float32)[:, None, None]
        + jnp.arange(STEPS, dtype=jnp.float32)[None, :, None]
        + jnp.zeros((1, 1, BEAMS), jnp.float32)
    ).reshape(row_count)
    frequency = rope_base ** (-2.0 * jnp.arange(ROPE // 2, dtype=jnp.float32) / ROPE)
    angles = positions[:, None] * frequency[None, :]
    cos_val = jnp.cos(angles)
    sin_val = jnp.sin(angles)
    queries = jnp.dot(normed, w_query, preferred_element_type=jnp.float32).reshape(
        row_count, heads_local, NOPE + ROPE
    )
    q_nope = queries[:, :, :NOPE].astype(jnp.bfloat16)
    q_rope = rotate(queries[:, :, NOPE:], cos_val[:, None, :], sin_val[:, None, :]).astype(
        jnp.bfloat16
    )
    kv_part = jnp.dot(normed, w_latent, preferred_element_type=jnp.float32)
    kv_all = lax.all_gather(kv_part, "tp", axis=1, tiled=True)
    new_lat = kv_all[:, :LATENT] * rms_scale(kv_all[:, :LATENT]) * kv_gain
    new_rope = rotate(kv_all[:, LATENT:], cos_val, sin_val)
    new_keys = jnp.concatenate([new_lat, new_rope], axis=1).astype(jnp.bfloat16)
    key_up = w_key_up.reshape(LATENT, heads_local, NOPE)
    q_lat = jnp.einsum("nhc,lhc->nhl", q_nope, key_up, preferred_element_type=jnp.float32).astype(
        jnp.bfloat16
    )
    query_key = jnp.concatenate([q_lat, q_rope], axis=2)
    pool_index = (jnp.arange(req_local, dtype=jnp.int32) * PAGES)[:, None] + page_table
    cache_keys = jnp.take(latent_cache, pool_index.reshape(-1), axis=0).reshape(
        req_local, max_len, LATENT + ROPE
    )
    live_mask = jnp.arange(max_len, dtype=jnp.int32)[None, :] < cache_len[:, None]
    score_scale = (NOPE + ROPE) ** (-0.5)
    grouped = query_key.reshape(req_local, STEPS * BEAMS * heads_local, LATENT + ROPE)
    s_cache = (
        jnp.einsum("rqd,rld->rql", grouped, cache_keys, preferred_element_type=jnp.float32)
        * score_scale
    )
    s_cache = jnp.where(live_mask[:, None, :], s_cache, -jnp.inf).reshape(
        req_local, STEPS, BEAMS, heads_local, max_len
    )
    fresh = new_keys.reshape(req_local, STEPS, BEAMS, LATENT + ROPE).astype(jnp.float32)
    parent_hot = (parents[..., None] == jnp.arange(BEAMS, dtype=jnp.int32)).astype(jnp.float32)
    identity = jnp.broadcast_to(jnp.eye(BEAMS, dtype=jnp.float32), (req_local, BEAMS, BEAMS))
    tail_rows = []
    for step_index in range(STEPS):
        lineage = identity
        pieces = [None] * STEPS
        for earlier in range(step_index, -1, -1):
            pieces[earlier] = jnp.einsum(
                "rba,rad->rbd", lineage, fresh[:, earlier], precision=highest
            )
            if earlier > 0:
                lineage = jnp.einsum(
                    "rba,rac->rbc", lineage, parent_hot[:, earlier - 1], precision=highest
                )
        for later in range(step_index + 1, STEPS):
            pieces[later] = jnp.zeros_like(pieces[0])
        tail_rows.append(jnp.stack(pieces, axis=2))
    tail_keys = jnp.stack(tail_rows, axis=1).astype(jnp.bfloat16)
    queries_tail = query_key.reshape(req_local, STEPS, BEAMS, heads_local, LATENT + ROPE)
    s_tail = (
        jnp.einsum(
            "rsbhd,rsbjd->rsbhj", queries_tail, tail_keys, preferred_element_type=jnp.float32
        )
        * score_scale
    )
    causal = jnp.arange(STEPS)[None, :] <= jnp.arange(STEPS)[:, None]
    s_tail = jnp.where(causal[None, :, None, None, :], s_tail, -jnp.inf)
    top_score = jnp.maximum(jnp.max(s_cache, axis=-1), jnp.max(s_tail, axis=-1))
    e_cache = jnp.exp(s_cache - top_score[..., None])
    e_tail = jnp.exp(s_tail - top_score[..., None])
    total = jnp.sum(e_cache, axis=-1) + jnp.sum(e_tail, axis=-1)
    p_cache = (e_cache / total[..., None]).astype(jnp.bfloat16)
    p_tail = (e_tail / total[..., None]).astype(jnp.bfloat16)
    context = jnp.einsum(
        "rsbhl,rld->rsbhd", p_cache, cache_keys[..., :LATENT], preferred_element_type=jnp.float32
    )
    context = context + jnp.einsum(
        "rsbhj,rsbjd->rsbhd", p_tail, tail_keys[..., :LATENT], preferred_element_type=jnp.float32
    )
    context = context.astype(jnp.bfloat16).reshape(row_count, heads_local, LATENT)
    value_up = w_value_up.reshape(LATENT, heads_local, VDIM)
    head_out = (
        jnp.einsum("nhl,lhv->nhv", context, value_up, preferred_element_type=jnp.float32)
        .astype(jnp.bfloat16)
        .reshape(row_count, heads_local * VDIM)
    )
    attn_part = jnp.dot(head_out, w_out, preferred_element_type=jnp.float32)
    expert_count = EXP_DEV * req_count
    capacity = min(row_count, 2 * row_count * TOPK // expert_count)
    slot_count = expert_count * capacity
    picks = routes.reshape(-1)
    pick_hot = (picks[:, None] == jnp.arange(expert_count, dtype=jnp.int32)[None, :]).astype(
        jnp.int32
    )
    before = jnp.cumsum(pick_hot, axis=0) - pick_hot
    ranks = jnp.sum(before * pick_hot, axis=1)
    slot_of = picks * capacity + ranks
    slot_hot = (slot_of[:, None] == jnp.arange(slot_count, dtype=jnp.int32)[None, :]).reshape(
        row_count, TOPK, slot_count
    )
    gather_rows = jnp.sum(slot_hot.astype(jnp.int32), axis=1).astype(jnp.bfloat16)
    weight_rows = jnp.sum(jnp.where(slot_hot, route_weights[:, :, None], 0.0), axis=1)
    tp_index = lax.axis_index("tp")
    col_start = tp_index * col_share
    attn_part, down_cols = lax.optimization_barrier((attn_part, down_by_columns(w_down)))
    attn_cols = lax.psum_scatter(attn_part, "tp", scatter_dimension=1, tiled=True)
    hidden_cols = lax.dynamic_slice_in_dim(hidden_f, col_start, col_share, 1)
    resid_cols = hidden_cols + attn_cols
    square_sum = lax.psum(jnp.sum(resid_cols * resid_cols, axis=-1, keepdims=True), "tp")
    moe_scale = lax.rsqrt(square_sum / D + eps)
    gain_cols = lax.dynamic_slice_in_dim(moe_gain, col_start, col_share, 0)
    moe_in_cols = (resid_cols * moe_scale * gain_cols).astype(jnp.bfloat16)
    placed = jnp.dot(gather_rows.T, moe_in_cols, preferred_element_type=jnp.float32).astype(
        jnp.bfloat16
    )
    arrived_cols = lax.all_to_all(
        placed.reshape(req_count, EXP_DEV, capacity, col_share),
        "req",
        split_axis=0,
        concat_axis=0,
        tiled=True,
    )
    arrived = lax.all_gather(arrived_cols, "tp", axis=3, tiled=True)
    shares = expert_math(arrived, w_gate, w_up, down_cols)
    returned = send_home(shares)
    combined = jnp.dot(
        weight_rows, returned.reshape(slot_count, col_share).astype(jnp.float32), precision=highest
    )
    return (resid_cols + combined).astype(jnp.bfloat16)


def solution(mesh):
    in_specs = (
        P("req", None),
        P(),
        P(None, "tp"),
        P(None, "tp"),
        P(),
        P(None, "tp"),
        P(None, "tp"),
        P("tp", None),
        P(),
        P("req", None, "tp"),
        P("req", None, "tp"),
        P("req", "tp", None),
        P("req", None, None),
        P("req", None),
        P("req"),
        P("req", None, None),
        P("req", None),
        P("req", None),
    )
    out_specs = P("req", "tp")
    return jax.shard_map(local, mesh=mesh, in_specs=in_specs, out_specs=out_specs, check_vma=False)
```

```python
import jax
import jax.numpy as jnp
from jax import lax
from jax.sharding import PartitionSpec as P

D = 2048
NOPE = 128
ROPE = 64
VDIM = 128
LATENT = 512
TOPK = 6
EXP_DEV = 1
BEAMS = 8
STEPS = 4
PAGE = 64
PAGES = 8


eps = 1e-06
rope_base = 50000.0


def rms_scale(values):
    return lax.rsqrt(jnp.mean(values * values, axis=-1, keepdims=True) + eps)


def rotate(values, cos_val, sin_val):
    half_rope = values.shape[-1] // 2
    first = values[..., :half_rope]
    second = values[..., half_rope:]
    return jnp.concatenate(
        [first * cos_val - second * sin_val, second * cos_val + first * sin_val], axis=-1
    )


def expert_math(arrived, gate_w, up_w, down_cols):
    gate_val = jnp.einsum("nesd,edf->nesf", arrived, gate_w, preferred_element_type=jnp.float32)
    up_val = jnp.einsum("nesd,edf->nesf", arrived, up_w, preferred_element_type=jnp.float32)
    active = (jax.nn.silu(gate_val) * up_val).astype(jnp.bfloat16)
    active_all = lax.all_gather(active, "tp", axis=0)
    return jnp.einsum(
        "tnesf,etfd->nesd", active_all, down_cols, preferred_element_type=jnp.float32
    ).astype(jnp.bfloat16)


def down_by_columns(down_w):
    tp_count = lax.axis_size("tp")
    tp_index = lax.axis_index("tp")
    col_share = down_w.shape[2] // tp_count
    pieces = [None] * tp_count
    for shift in range(tp_count):
        target = (tp_index + shift) % tp_count
        piece = lax.dynamic_slice_in_dim(down_w, target * col_share, col_share, 2)
        if shift:
            piece = lax.ppermute(
                piece, "tp", [(s, (s + shift) % tp_count) for s in range(tp_count)]
            )
        pieces[shift] = piece
    stacked = jnp.stack(pieces, axis=1)
    return jnp.take(stacked, (tp_index - jnp.arange(tp_count)) % tp_count, axis=1)


def send_home(shares):
    return lax.all_to_all(shares, "req", split_axis=0, concat_axis=0, tiled=True)


def local(
    hidden_in,
    attn_gain,
    w_query,
    w_latent,
    kv_gain,
    w_key_up,
    w_value_up,
    w_out,
    moe_gain,
    w_gate,
    w_up,
    w_down,
    latent_cache,
    page_table,
    cache_len,
    parents,
    routes,
    route_weights,
):
    highest = lax.Precision.HIGHEST
    row_count = hidden_in.shape[0]
    req_local = cache_len.shape[0]
    heads_local = w_value_up.shape[1] // VDIM
    tp_count = lax.axis_size("tp")
    req_count = lax.axis_size("req")
    col_share = D // tp_count
    max_len = PAGES * PAGE
    hidden_f = hidden_in.astype(jnp.float32)
    normed = (hidden_f * rms_scale(hidden_f) * attn_gain).astype(jnp.bfloat16)
    positions = (
        cache_len.astype(jnp.float32)[:, None, None]
        + jnp.arange(STEPS, dtype=jnp.float32)[None, :, None]
        + jnp.zeros((1, 1, BEAMS), jnp.float32)
    ).reshape(row_count)
    frequency = rope_base ** (-2.0 * jnp.arange(ROPE // 2, dtype=jnp.float32) / ROPE)
    angles = positions[:, None] * frequency[None, :]
    cos_val = jnp.cos(angles)
    sin_val = jnp.sin(angles)
    queries = jnp.dot(normed, w_query, preferred_element_type=jnp.float32).reshape(
        row_count, heads_local, NOPE + ROPE
    )
    q_nope = queries[:, :, :NOPE].astype(jnp.bfloat16)
    q_rope = rotate(queries[:, :, NOPE:], cos_val[:, None, :], sin_val[:, None, :]).astype(
        jnp.bfloat16
    )
    kv_part = jnp.dot(normed, w_latent, preferred_element_type=jnp.float32)
    kv_all = lax.all_gather(kv_part, "tp", axis=1, tiled=True)
    new_lat = kv_all[:, :LATENT] * rms_scale(kv_all[:, :LATENT]) * kv_gain
    new_rope = rotate(kv_all[:, LATENT:], cos_val, sin_val)
    new_keys = jnp.concatenate([new_lat, new_rope], axis=1).astype(jnp.bfloat16)
    key_up = w_key_up.reshape(LATENT, heads_local, NOPE)
    q_lat = jnp.einsum("nhc,lhc->nhl", q_nope, key_up, preferred_element_type=jnp.float32).astype(
        jnp.bfloat16
    )
    query_key = jnp.concatenate([q_lat, q_rope], axis=2)
    pool_index = (jnp.arange(req_local, dtype=jnp.int32) * PAGES)[:, None] + page_table
    cache_keys = jnp.take(latent_cache, pool_index.reshape(-1), axis=0).reshape(
        req_local, max_len, LATENT + ROPE
    )
    live_mask = jnp.arange(max_len, dtype=jnp.int32)[None, :] < cache_len[:, None]
    score_scale = (NOPE + ROPE) ** (-0.5)
    grouped = query_key.reshape(req_local, STEPS * BEAMS * heads_local, LATENT + ROPE)
    s_cache = (
        jnp.einsum("rqd,rld->rql", grouped, cache_keys, preferred_element_type=jnp.float32)
        * score_scale
    )
    s_cache = jnp.where(live_mask[:, None, :], s_cache, -jnp.inf).reshape(
        req_local, STEPS, BEAMS, heads_local, max_len
    )
    fresh = new_keys.reshape(req_local, STEPS, BEAMS, LATENT + ROPE).astype(jnp.float32)
    parent_hot = (parents[..., None] == jnp.arange(BEAMS, dtype=jnp.int32)).astype(jnp.float32)
    identity = jnp.broadcast_to(jnp.eye(BEAMS, dtype=jnp.float32), (req_local, BEAMS, BEAMS))
    tail_rows = []
    for step_index in range(STEPS):
        lineage = identity
        pieces = [None] * STEPS
        for earlier in range(step_index, -1, -1):
            pieces[earlier] = jnp.einsum(
                "rba,rad->rbd", lineage, fresh[:, earlier], precision=highest
            )
            if earlier > 0:
                lineage = jnp.einsum(
                    "rba,rac->rbc", lineage, parent_hot[:, earlier - 1], precision=highest
                )
        for later in range(step_index + 1, STEPS):
            pieces[later] = jnp.zeros_like(pieces[0])
        tail_rows.append(jnp.stack(pieces, axis=2))
    tail_keys = jnp.stack(tail_rows, axis=1).astype(jnp.bfloat16)
    queries_tail = query_key.reshape(req_local, STEPS, BEAMS, heads_local, LATENT + ROPE)
    s_tail = (
        jnp.einsum(
            "rsbhd,rsbjd->rsbhj", queries_tail, tail_keys, preferred_element_type=jnp.float32
        )
        * score_scale
    )
    causal = jnp.arange(STEPS)[None, :] <= jnp.arange(STEPS)[:, None]
    s_tail = jnp.where(causal[None, :, None, None, :], s_tail, -jnp.inf)
    top_score = jnp.maximum(jnp.max(s_cache, axis=-1), jnp.max(s_tail, axis=-1))
    e_cache = jnp.exp(s_cache - top_score[..., None])
    e_tail = jnp.exp(s_tail - top_score[..., None])
    total = jnp.sum(e_cache, axis=-1) + jnp.sum(e_tail, axis=-1)
    p_cache = (e_cache / total[..., None]).astype(jnp.bfloat16)
    p_tail = (e_tail / total[..., None]).astype(jnp.bfloat16)
    context = jnp.einsum(
        "rsbhl,rld->rsbhd", p_cache, cache_keys[..., :LATENT], preferred_element_type=jnp.float32
    )
    context = context + jnp.einsum(
        "rsbhj,rsbjd->rsbhd", p_tail, tail_keys[..., :LATENT], preferred_element_type=jnp.float32
    )
    context = context.astype(jnp.bfloat16).reshape(row_count, heads_local, LATENT)
    value_up = w_value_up.reshape(LATENT, heads_local, VDIM)
    head_out = (
        jnp.einsum("nhl,lhv->nhv", context, value_up, preferred_element_type=jnp.float32)
        .astype(jnp.bfloat16)
        .reshape(row_count, heads_local * VDIM)
    )
    attn_part = jnp.dot(head_out, w_out, preferred_element_type=jnp.float32)
    expert_count = EXP_DEV * req_count
    capacity = min(row_count, 2 * row_count * TOPK // expert_count)
    slot_count = expert_count * capacity
    picks = routes.reshape(-1)
    pick_hot = (picks[:, None] == jnp.arange(expert_count, dtype=jnp.int32)[None, :]).astype(
        jnp.int32
    )
    before = jnp.cumsum(pick_hot, axis=0) - pick_hot
    ranks = jnp.sum(before * pick_hot, axis=1)
    slot_of = picks * capacity + ranks
    slot_hot = (slot_of[:, None] == jnp.arange(slot_count, dtype=jnp.int32)[None, :]).reshape(
        row_count, TOPK, slot_count
    )
    gather_rows = jnp.sum(slot_hot.astype(jnp.int32), axis=1).astype(jnp.bfloat16)
    weight_rows = jnp.sum(jnp.where(slot_hot, route_weights[:, :, None], 0.0), axis=1)
    tp_index = lax.axis_index("tp")
    col_start = tp_index * col_share
    attn_part, down_cols = lax.optimization_barrier((attn_part, down_by_columns(w_down)))
    attn_cols = lax.psum_scatter(attn_part, "tp", scatter_dimension=1, tiled=True)
    hidden_cols = lax.dynamic_slice_in_dim(hidden_f, col_start, col_share, 1)
    resid_cols = hidden_cols + attn_cols
    square_sum = lax.psum(jnp.sum(resid_cols * resid_cols, axis=-1, keepdims=True), "tp")
    moe_scale = lax.rsqrt(square_sum / D + eps)
    gain_cols = lax.dynamic_slice_in_dim(moe_gain, col_start, col_share, 0)
    moe_in_cols = (resid_cols * moe_scale * gain_cols).astype(jnp.bfloat16)
    placed = jnp.dot(gather_rows.T, moe_in_cols, preferred_element_type=jnp.float32).astype(
        jnp.bfloat16
    )
    arrived_cols = lax.all_to_all(
        placed.reshape(req_count, EXP_DEV, capacity, col_share),
        "req",
        split_axis=0,
        concat_axis=0,
        tiled=True,
    )
    arrived = lax.all_gather(arrived_cols, "tp", axis=3, tiled=True)
    shares = expert_math(arrived, w_gate, w_up, down_cols)
    returned = send_home(shares)
    combined = jnp.dot(
        weight_rows, returned.reshape(slot_count, col_share).astype(jnp.float32), precision=highest
    )
    return (resid_cols + combined).astype(jnp.bfloat16)


def solution(mesh):
    in_specs = (
        P("req", None),
        P(),
        P(None, "tp"),
        P(None, "tp"),
        P(),
        P(None, "tp"),
        P(None, "tp"),
        P("tp", None),
        P(),
        P("req", None, "tp"),
        P("req", None, "tp"),
        P("req", "tp", None),
        P("req", None, None),
        P("req", None),
        P("req"),
        P("req", None, None),
        P("req", None),
        P("req", None),
    )
    out_specs = P("req", "tp")
    return jax.shard_map(local, mesh=mesh, in_specs=in_specs, out_specs=out_specs, check_vma=False)
```

```python
import jax
import jax.numpy as jnp
from jax import lax
from jax.sharding import PartitionSpec as P

D = 2048
NOPE = 128
ROPE = 64
VDIM = 128
LATENT = 512
TOPK = 6
EXP_DEV = 1
BEAMS = 8
STEPS = 4
PAGE = 64
PAGES = 8


eps = 1e-06
rope_base = 50000.0


def rms_scale(values):
    return lax.rsqrt(jnp.mean(values * values, axis=-1, keepdims=True) + eps)


def rotate(values, cos_val, sin_val):
    half_rope = values.shape[-1] // 2
    first = values[..., :half_rope]
    second = values[..., half_rope:]
    return jnp.concatenate(
        [first * cos_val - second * sin_val, second * cos_val + first * sin_val], axis=-1
    )


def expert_math(arrived, gate_w, up_w, down_cols):
    gate_val = jnp.einsum("nesd,edf->nesf", arrived, gate_w, preferred_element_type=jnp.float32)
    up_val = jnp.einsum("nesd,edf->nesf", arrived, up_w, preferred_element_type=jnp.float32)
    active = (jax.nn.silu(gate_val) * up_val).astype(jnp.bfloat16)
    active_all = lax.all_gather(active, "tp", axis=0)
    return jnp.einsum(
        "tnesf,etfd->nesd", active_all, down_cols, preferred_element_type=jnp.float32
    ).astype(jnp.bfloat16)


def down_by_columns(down_w):
    tp_count = lax.axis_size("tp")
    tp_index = lax.axis_index("tp")
    col_share = down_w.shape[2] // tp_count
    pieces = [None] * tp_count
    for shift in range(tp_count):
        target = (tp_index + shift) % tp_count
        piece = lax.dynamic_slice_in_dim(down_w, target * col_share, col_share, 2)
        if shift:
            piece = lax.ppermute(
                piece, "tp", [(s, (s + shift) % tp_count) for s in range(tp_count)]
            )
        pieces[shift] = piece
    stacked = jnp.stack(pieces, axis=1)
    return jnp.take(stacked, (tp_index - jnp.arange(tp_count)) % tp_count, axis=1)


def send_home(shares):
    return lax.all_to_all(shares, "req", split_axis=0, concat_axis=0, tiled=True)


def local(
    hidden_in,
    attn_gain,
    w_query,
    w_latent,
    kv_gain,
    w_key_up,
    w_value_up,
    w_out,
    moe_gain,
    w_gate,
    w_up,
    w_down,
    latent_cache,
    page_table,
    cache_len,
    parents,
    routes,
    route_weights,
):
    highest = lax.Precision.HIGHEST
    row_count = hidden_in.shape[0]
    req_local = cache_len.shape[0]
    heads_local = w_value_up.shape[1] // VDIM
    tp_count = lax.axis_size("tp")
    req_count = lax.axis_size("req")
    col_share = D // tp_count
    max_len = PAGES * PAGE
    hidden_f = hidden_in.astype(jnp.float32)
    normed = (hidden_f * rms_scale(hidden_f) * attn_gain).astype(jnp.bfloat16)
    positions = (
        cache_len.astype(jnp.float32)[:, None, None]
        + jnp.arange(STEPS, dtype=jnp.float32)[None, :, None]
        + jnp.zeros((1, 1, BEAMS), jnp.float32)
    ).reshape(row_count)
    frequency = rope_base ** (-2.0 * jnp.arange(ROPE // 2, dtype=jnp.float32) / ROPE)
    angles = positions[:, None] * frequency[None, :]
    cos_val = jnp.cos(angles)
    sin_val = jnp.sin(angles)
    queries = jnp.dot(normed, w_query, preferred_element_type=jnp.float32).reshape(
        row_count, heads_local, NOPE + ROPE
    )
    q_nope = queries[:, :, :NOPE].astype(jnp.bfloat16)
    q_rope = rotate(queries[:, :, NOPE:], cos_val[:, None, :], sin_val[:, None, :]).astype(
        jnp.bfloat16
    )
    kv_part = jnp.dot(normed, w_latent, preferred_element_type=jnp.float32)
    kv_all = lax.all_gather(kv_part, "tp", axis=1, tiled=True)
    kv_all, down_late = lax.optimization_barrier((kv_all, w_down))
    new_lat = kv_all[:, :LATENT] * rms_scale(kv_all[:, :LATENT]) * kv_gain
    new_rope = rotate(kv_all[:, LATENT:], cos_val, sin_val)
    new_keys = jnp.concatenate([new_lat, new_rope], axis=1).astype(jnp.bfloat16)
    key_up = w_key_up.reshape(LATENT, heads_local, NOPE)
    q_lat = jnp.einsum("nhc,lhc->nhl", q_nope, key_up, preferred_element_type=jnp.float32).astype(
        jnp.bfloat16
    )
    query_key = jnp.concatenate([q_lat, q_rope], axis=2)
    cache_keys = latent_cache.reshape(req_local, max_len, LATENT + ROPE)
    page_hot = page_table[:, :, None] == jnp.arange(PAGES, dtype=jnp.int32)[None, None, :]
    logical_page = jnp.sum(
        jnp.where(page_hot, jnp.arange(PAGES, dtype=jnp.int32)[None, :, None], 0), axis=1
    )
    logical_pos = (
        logical_page[:, :, None] * PAGE + jnp.arange(PAGE, dtype=jnp.int32)[None, None, :]
    ).reshape(req_local, max_len)
    live_mask = logical_pos < cache_len[:, None]
    score_scale = (NOPE + ROPE) ** (-0.5)
    grouped = query_key.reshape(req_local, STEPS * BEAMS * heads_local, LATENT + ROPE)
    s_cache = (
        jnp.einsum("rqd,rld->rql", grouped, cache_keys, preferred_element_type=jnp.float32)
        * score_scale
    )
    s_cache = jnp.where(live_mask[:, None, :], s_cache, -jnp.inf).reshape(
        req_local, STEPS, BEAMS, heads_local, max_len
    )
    fresh = new_keys.reshape(req_local, STEPS, BEAMS, LATENT + ROPE)
    beam_ids = jnp.arange(BEAMS, dtype=jnp.int32)
    lineage_rows = []
    for step_index in range(STEPS):
        lineage = jnp.broadcast_to(beam_ids[None, :], (req_local, BEAMS))
        pieces = [None] * STEPS
        for earlier in range(step_index, -1, -1):
            pieces[earlier] = lineage
            if earlier > 0:
                lineage_hot = lineage[:, :, None] == beam_ids[None, None, :]
                lineage = jnp.sum(
                    jnp.where(lineage_hot, parents[:, earlier - 1][:, None, :], 0), axis=2
                )
        for later in range(step_index + 1, STEPS):
            pieces[later] = jnp.full((req_local, BEAMS), -1, jnp.int32)
        lineage_rows.append(jnp.stack(pieces, axis=2))
    lineage_all = jnp.stack(lineage_rows, axis=1)
    pick = (lineage_all[..., None] == beam_ids).astype(jnp.bfloat16)
    tail_keys = jnp.einsum(
        "rsbja,rjad->rsbjd", pick, fresh, preferred_element_type=jnp.float32
    ).astype(jnp.bfloat16)
    queries_tail = query_key.reshape(req_local, STEPS, BEAMS, heads_local, LATENT + ROPE)
    s_tail = (
        jnp.einsum(
            "rsbhd,rsbjd->rsbhj", queries_tail, tail_keys, preferred_element_type=jnp.float32
        )
        * score_scale
    )
    causal = jnp.arange(STEPS)[None, :] <= jnp.arange(STEPS)[:, None]
    s_tail = jnp.where(causal[None, :, None, None, :], s_tail, -jnp.inf)
    top_score = jnp.maximum(jnp.max(s_cache, axis=-1), jnp.max(s_tail, axis=-1))
    e_cache = jnp.exp(s_cache - top_score[..., None])
    e_tail = jnp.exp(s_tail - top_score[..., None])
    total = jnp.sum(e_cache, axis=-1) + jnp.sum(e_tail, axis=-1)
    p_cache = (e_cache / total[..., None]).astype(jnp.bfloat16)
    p_tail = (e_tail / total[..., None]).astype(jnp.bfloat16)
    context = jnp.einsum(
        "rsbhl,rld->rsbhd", p_cache, cache_keys[..., :LATENT], preferred_element_type=jnp.float32
    )
    context = context + jnp.einsum(
        "rsbhj,rsbjd->rsbhd", p_tail, tail_keys[..., :LATENT], preferred_element_type=jnp.float32
    )
    context = context.astype(jnp.bfloat16).reshape(row_count, heads_local, LATENT)
    value_up = w_value_up.reshape(LATENT, heads_local, VDIM)
    head_out = (
        jnp.einsum("nhl,lhv->nhv", context, value_up, preferred_element_type=jnp.float32)
        .astype(jnp.bfloat16)
        .reshape(row_count, heads_local * VDIM)
    )
    attn_part = jnp.dot(head_out, w_out, preferred_element_type=jnp.float32)
    expert_count = EXP_DEV * req_count
    capacity = min(row_count, 2 * row_count * TOPK // expert_count)
    slot_count = expert_count * capacity
    picks = routes.reshape(-1)
    pick_hot = (picks[:, None] == jnp.arange(expert_count, dtype=jnp.int32)[None, :]).astype(
        jnp.int32
    )
    before = jnp.cumsum(pick_hot, axis=0) - pick_hot
    ranks = jnp.sum(before * pick_hot, axis=1)
    slot_of = picks * capacity + ranks
    slot_hot = (slot_of[:, None] == jnp.arange(slot_count, dtype=jnp.int32)[None, :]).reshape(
        row_count, TOPK, slot_count
    )
    gather_rows = jnp.sum(slot_hot.astype(jnp.int32), axis=1).astype(jnp.bfloat16)
    weight_rows = jnp.sum(jnp.where(slot_hot, route_weights[:, :, None], 0.0), axis=1)
    tp_index = lax.axis_index("tp")
    col_start = tp_index * col_share
    attn_part, down_cols = lax.optimization_barrier((attn_part, down_by_columns(down_late)))
    attn_cols = lax.psum_scatter(attn_part, "tp", scatter_dimension=1, tiled=True)
    hidden_cols = lax.dynamic_slice_in_dim(hidden_f, col_start, col_share, 1)
    resid_cols = hidden_cols + attn_cols
    square_sum = lax.psum(jnp.sum(resid_cols * resid_cols, axis=-1, keepdims=True), "tp")
    moe_scale = lax.rsqrt(square_sum / D + eps)
    gain_cols = lax.dynamic_slice_in_dim(moe_gain, col_start, col_share, 0)
    moe_in_cols = (resid_cols * moe_scale * gain_cols).astype(jnp.bfloat16)
    placed = jnp.dot(gather_rows.T, moe_in_cols, preferred_element_type=jnp.float32).astype(
        jnp.bfloat16
    )
    arrived_cols = lax.all_to_all(
        placed.reshape(req_count, EXP_DEV, capacity, col_share),
        "req",
        split_axis=0,
        concat_axis=0,
        tiled=True,
    )
    arrived = lax.all_gather(arrived_cols, "tp", axis=3, tiled=True)
    shares = expert_math(arrived, w_gate, w_up, down_cols)
    returned = send_home(shares)
    combined = jnp.dot(
        weight_rows, returned.reshape(slot_count, col_share).astype(jnp.float32), precision=highest
    )
    return (resid_cols + combined).astype(jnp.bfloat16)


def solution(mesh):
    in_specs = (
        P("req", None),
        P(),
        P(None, "tp"),
        P(None, "tp"),
        P(),
        P(None, "tp"),
        P(None, "tp"),
        P("tp", None),
        P(),
        P("req", None, "tp"),
        P("req", None, "tp"),
        P("req", "tp", None),
        P("req", None, None),
        P("req", None),
        P("req"),
        P("req", None, None),
        P("req", None),
        P("req", None),
    )
    out_specs = P("req", "tp")
    return jax.shard_map(local, mesh=mesh, in_specs=in_specs, out_specs=out_specs, check_vma=False)
```

```python
import jax
import jax.numpy as jnp
from jax import lax
from jax.sharding import PartitionSpec as P

D = 2048
NOPE = 128
ROPE = 64
VDIM = 128
LATENT = 512
TOPK = 6
EXP_DEV = 1
BEAMS = 8
STEPS = 4
PAGE = 64
PAGES = 8


eps = 1e-06
rope_base = 50000.0


def rms_scale(values):
    return lax.rsqrt(jnp.mean(values * values, axis=-1, keepdims=True) + eps)


def rotate(values, cos_val, sin_val):
    half_rope = values.shape[-1] // 2
    first = values[..., :half_rope]
    second = values[..., half_rope:]
    return jnp.concatenate(
        [first * cos_val - second * sin_val, second * cos_val + first * sin_val], axis=-1
    )


def expert_math(arrived, gate_w, up_w, down_cols):
    gate_val = jnp.einsum("nesd,edf->nesf", arrived, gate_w, preferred_element_type=jnp.float32)
    up_val = jnp.einsum("nesd,edf->nesf", arrived, up_w, preferred_element_type=jnp.float32)
    active = (jax.nn.silu(gate_val) * up_val).astype(jnp.bfloat16)
    active_all = lax.all_gather(active, "tp", axis=0)
    return jnp.einsum(
        "tnesf,etfd->nesd", active_all, down_cols, preferred_element_type=jnp.float32
    ).astype(jnp.bfloat16)


def down_by_columns(down_w):
    tp_count = lax.axis_size("tp")
    tp_index = lax.axis_index("tp")
    col_share = down_w.shape[2] // tp_count
    pieces = [None] * tp_count
    for shift in range(tp_count):
        target = (tp_index + shift) % tp_count
        piece = lax.dynamic_slice_in_dim(down_w, target * col_share, col_share, 2)
        if shift:
            piece = lax.ppermute(
                piece, "tp", [(s, (s + shift) % tp_count) for s in range(tp_count)]
            )
        pieces[shift] = piece
    reverse = [pieces[(-shift) % tp_count] for shift in range(tp_count)]
    doubled = jnp.stack(reverse + reverse, axis=1)
    start = (tp_count - tp_index) % tp_count
    return lax.dynamic_slice_in_dim(doubled, start, tp_count, 1)


def send_home(shares):
    return lax.all_to_all(shares, "req", split_axis=0, concat_axis=0, tiled=True)


def local(
    hidden_in,
    attn_gain,
    w_query,
    w_latent,
    kv_gain,
    w_key_up,
    w_value_up,
    w_out,
    moe_gain,
    w_gate,
    w_up,
    w_down,
    latent_cache,
    page_table,
    cache_len,
    parents,
    routes,
    route_weights,
):
    highest = lax.Precision.HIGHEST
    row_count = hidden_in.shape[0]
    req_local = cache_len.shape[0]
    heads_local = w_value_up.shape[1] // VDIM
    tp_count = lax.axis_size("tp")
    req_count = lax.axis_size("req")
    col_share = D // tp_count
    max_len = PAGES * PAGE
    hidden_f = hidden_in.astype(jnp.float32)
    normed = (hidden_f * rms_scale(hidden_f) * attn_gain).astype(jnp.bfloat16)
    positions = (
        cache_len.astype(jnp.float32)[:, None, None]
        + jnp.arange(STEPS, dtype=jnp.float32)[None, :, None]
        + jnp.zeros((1, 1, BEAMS), jnp.float32)
    ).reshape(row_count)
    frequency = rope_base ** (-2.0 * jnp.arange(ROPE // 2, dtype=jnp.float32) / ROPE)
    angles = positions[:, None] * frequency[None, :]
    cos_val = jnp.cos(angles)
    sin_val = jnp.sin(angles)
    queries = jnp.dot(normed, w_query, preferred_element_type=jnp.float32).reshape(
        row_count, heads_local, NOPE + ROPE
    )
    q_nope = queries[:, :, :NOPE].astype(jnp.bfloat16)
    q_rope = rotate(queries[:, :, NOPE:], cos_val[:, None, :], sin_val[:, None, :]).astype(
        jnp.bfloat16
    )
    kv_part = jnp.dot(normed, w_latent, preferred_element_type=jnp.float32)
    kv_all = lax.all_gather(kv_part, "tp", axis=1, tiled=True)
    kv_all, down_late, out_late = lax.optimization_barrier((kv_all, w_down, w_out))
    out_all = lax.all_gather(out_late, "tp", axis=0, tiled=True)
    new_lat = kv_all[:, :LATENT] * rms_scale(kv_all[:, :LATENT]) * kv_gain
    new_rope = rotate(kv_all[:, LATENT:], cos_val, sin_val)
    new_keys = jnp.concatenate([new_lat, new_rope], axis=1).astype(jnp.bfloat16)
    key_up = w_key_up.reshape(LATENT, heads_local, NOPE)
    q_lat = jnp.einsum("nhc,lhc->nhl", q_nope, key_up, preferred_element_type=jnp.float32).astype(
        jnp.bfloat16
    )
    query_key = jnp.concatenate([q_lat, q_rope], axis=2)
    cache_keys = latent_cache.reshape(req_local, max_len, LATENT + ROPE)
    page_hot = page_table[:, :, None] == jnp.arange(PAGES, dtype=jnp.int32)[None, None, :]
    logical_page = jnp.sum(
        jnp.where(page_hot, jnp.arange(PAGES, dtype=jnp.int32)[None, :, None], 0), axis=1
    )
    logical_pos = (
        logical_page[:, :, None] * PAGE + jnp.arange(PAGE, dtype=jnp.int32)[None, None, :]
    ).reshape(req_local, max_len)
    live_mask = logical_pos < cache_len[:, None]
    score_scale = (NOPE + ROPE) ** (-0.5)
    grouped = query_key.reshape(req_local, STEPS * BEAMS * heads_local, LATENT + ROPE)
    s_cache = (
        jnp.einsum("rqd,rld->rql", grouped, cache_keys, preferred_element_type=jnp.float32)
        * score_scale
    )
    s_cache = jnp.where(live_mask[:, None, :], s_cache, -jnp.inf).reshape(
        req_local, STEPS, BEAMS, heads_local, max_len
    )
    fresh = new_keys.reshape(req_local, STEPS, BEAMS, LATENT + ROPE)
    beam_ids = jnp.arange(BEAMS, dtype=jnp.int32)
    lineage_rows = []
    for step_index in range(STEPS):
        lineage = jnp.broadcast_to(beam_ids[None, :], (req_local, BEAMS))
        pieces = [None] * STEPS
        for earlier in range(step_index, -1, -1):
            pieces[earlier] = lineage
            if earlier > 0:
                lineage_hot = lineage[:, :, None] == beam_ids[None, None, :]
                lineage = jnp.sum(
                    jnp.where(lineage_hot, parents[:, earlier - 1][:, None, :], 0), axis=2
                )
        for later in range(step_index + 1, STEPS):
            pieces[later] = jnp.full((req_local, BEAMS), -1, jnp.int32)
        lineage_rows.append(jnp.stack(pieces, axis=2))
    lineage_all = jnp.stack(lineage_rows, axis=1)
    pick = (lineage_all[..., None] == beam_ids).astype(jnp.bfloat16)
    tail_keys = jnp.einsum(
        "rsbja,rjad->rsbjd", pick, fresh, preferred_element_type=jnp.float32
    ).astype(jnp.bfloat16)
    queries_tail = query_key.reshape(req_local, STEPS, BEAMS, heads_local, LATENT + ROPE)
    s_tail = (
        jnp.einsum(
            "rsbhd,rsbjd->rsbhj", queries_tail, tail_keys, preferred_element_type=jnp.float32
        )
        * score_scale
    )
    causal = jnp.arange(STEPS)[None, :] <= jnp.arange(STEPS)[:, None]
    s_tail = jnp.where(causal[None, :, None, None, :], s_tail, -jnp.inf)
    top_score = jnp.maximum(jnp.max(s_cache, axis=-1), jnp.max(s_tail, axis=-1))
    e_cache = jnp.exp(s_cache - top_score[..., None])
    e_tail = jnp.exp(s_tail - top_score[..., None])
    total = jnp.sum(e_cache, axis=-1) + jnp.sum(e_tail, axis=-1)
    p_cache = (e_cache / total[..., None]).astype(jnp.bfloat16)
    p_tail = (e_tail / total[..., None]).astype(jnp.bfloat16)
    context = jnp.einsum(
        "rsbhl,rld->rsbhd", p_cache, cache_keys[..., :LATENT], preferred_element_type=jnp.float32
    )
    context = context + jnp.einsum(
        "rsbhj,rsbjd->rsbhd", p_tail, tail_keys[..., :LATENT], preferred_element_type=jnp.float32
    )
    context = context.astype(jnp.bfloat16).reshape(row_count, heads_local, LATENT)
    value_up = w_value_up.reshape(LATENT, heads_local, VDIM)
    head_out = (
        jnp.einsum("nhl,lhv->nhv", context, value_up, preferred_element_type=jnp.float32)
        .astype(jnp.bfloat16)
        .reshape(row_count, heads_local * VDIM)
    )
    expert_count = EXP_DEV * req_count
    capacity = min(row_count, 2 * row_count * TOPK // expert_count)
    slot_count = expert_count * capacity
    picks = routes.reshape(-1)
    pick_hot = (picks[:, None] == jnp.arange(expert_count, dtype=jnp.int32)[None, :]).astype(
        jnp.int32
    )
    before = jnp.cumsum(pick_hot, axis=0) - pick_hot
    ranks = jnp.sum(before * pick_hot, axis=1)
    slot_of = picks * capacity + ranks
    slot_hot = (slot_of[:, None] == jnp.arange(slot_count, dtype=jnp.int32)[None, :]).reshape(
        row_count, TOPK, slot_count
    )
    gather_rows = jnp.sum(slot_hot.astype(jnp.int32), axis=1).astype(jnp.bfloat16)
    weight_rows = jnp.sum(jnp.where(slot_hot, route_weights[:, :, None], 0.0), axis=1)
    tp_index = lax.axis_index("tp")
    col_start = tp_index * col_share
    head_all = lax.all_gather(head_out, "tp", axis=1, tiled=True)
    head_all, down_cols = lax.optimization_barrier((head_all, down_by_columns(down_late)))
    attn_full = jnp.dot(head_all, out_all, preferred_element_type=jnp.float32)
    resid_full = hidden_f + attn_full
    moe_in = (resid_full * rms_scale(resid_full) * moe_gain).astype(jnp.bfloat16)
    moe_in_cols = lax.dynamic_slice_in_dim(moe_in, col_start, col_share, 1)
    resid_cols = lax.dynamic_slice_in_dim(resid_full, col_start, col_share, 1)
    placed = jnp.dot(gather_rows.T, moe_in_cols, preferred_element_type=jnp.float32).astype(
        jnp.bfloat16
    )
    arrived_cols = lax.all_to_all(
        placed.reshape(req_count, EXP_DEV, capacity, col_share),
        "req",
        split_axis=0,
        concat_axis=0,
        tiled=True,
    )
    arrived = lax.all_gather(arrived_cols, "tp", axis=3, tiled=True)
    shares = expert_math(arrived, w_gate, w_up, down_cols)
    returned = send_home(shares)
    combined = jnp.dot(
        weight_rows, returned.reshape(slot_count, col_share).astype(jnp.float32), precision=highest
    )
    return (resid_cols + combined).astype(jnp.bfloat16)


def solution(mesh):
    in_specs = (
        P("req", None),
        P(),
        P(None, "tp"),
        P(None, "tp"),
        P(),
        P(None, "tp"),
        P(None, "tp"),
        P("tp", None),
        P(),
        P("req", None, "tp"),
        P("req", None, "tp"),
        P("req", "tp", None),
        P("req", None, None),
        P("req", None),
        P("req"),
        P("req", None, None),
        P("req", None),
        P("req", None),
    )
    out_specs = P("req", "tp")
    return jax.shard_map(local, mesh=mesh, in_specs=in_specs, out_specs=out_specs, check_vma=False)
```

```python
import jax
import jax.numpy as jnp
from jax import lax
from jax.sharding import PartitionSpec as P

D = 2048
NOPE = 128
ROPE = 64
VDIM = 128
LATENT = 512
TOPK = 6
EXP_DEV = 1
BEAMS = 8
STEPS = 4
PAGE = 64
PAGES = 8


eps = 1e-06
rope_base = 50000.0


def rms_scale(values):
    return lax.rsqrt(jnp.mean(values * values, axis=-1, keepdims=True) + eps)


def rotate(values, cos_val, sin_val):
    half_rope = values.shape[-1] // 2
    first = values[..., :half_rope]
    second = values[..., half_rope:]
    return jnp.concatenate(
        [first * cos_val - second * sin_val, second * cos_val + first * sin_val], axis=-1
    )


def expert_math(arrived, gate_w, up_w, down_cols):
    gate_val = jnp.einsum("nesd,edf->nesf", arrived, gate_w, preferred_element_type=jnp.float32)
    up_val = jnp.einsum("nesd,edf->nesf", arrived, up_w, preferred_element_type=jnp.float32)
    active = (jax.nn.silu(gate_val) * up_val).astype(jnp.bfloat16)
    active_all = lax.all_gather(active, "tp", axis=0)
    return jnp.einsum(
        "tnesf,etfd->nesd", active_all, down_cols, preferred_element_type=jnp.float32
    ).astype(jnp.bfloat16)


def by_columns(weight):
    tp_count = lax.axis_size("tp")
    tp_index = lax.axis_index("tp")
    col_share = weight.shape[-1] // tp_count
    pieces = [None] * tp_count
    for shift in range(tp_count):
        target = (tp_index + shift) % tp_count
        piece = lax.dynamic_slice_in_dim(weight, target * col_share, col_share, weight.ndim - 1)
        if shift:
            piece = lax.ppermute(
                piece, "tp", [(s, (s + shift) % tp_count) for s in range(tp_count)]
            )
        pieces[shift] = piece
    reverse = [pieces[(-shift) % tp_count] for shift in range(tp_count)]
    doubled = jnp.stack(reverse + reverse, axis=weight.ndim - 2)
    start = (tp_count - tp_index) % tp_count
    return lax.dynamic_slice_in_dim(doubled, start, tp_count, weight.ndim - 2)


def send_home(shares):
    return lax.all_to_all(shares, "req", split_axis=0, concat_axis=0, tiled=True)


def local(
    hidden_in,
    attn_gain,
    w_query,
    w_latent,
    kv_gain,
    w_key_up,
    w_value_up,
    w_out,
    moe_gain,
    w_gate,
    w_up,
    w_down,
    latent_cache,
    page_table,
    cache_len,
    parents,
    routes,
    route_weights,
):
    highest = lax.Precision.HIGHEST
    row_count = hidden_in.shape[0]
    req_local = cache_len.shape[0]
    heads_local = w_value_up.shape[1] // VDIM
    tp_count = lax.axis_size("tp")
    req_count = lax.axis_size("req")
    col_share = D // tp_count
    max_len = PAGES * PAGE
    hidden_f = hidden_in.astype(jnp.float32)
    normed = (hidden_f * rms_scale(hidden_f) * attn_gain).astype(jnp.bfloat16)
    positions = (
        cache_len.astype(jnp.float32)[:, None, None]
        + jnp.arange(STEPS, dtype=jnp.float32)[None, :, None]
        + jnp.zeros((1, 1, BEAMS), jnp.float32)
    ).reshape(row_count)
    frequency = rope_base ** (-2.0 * jnp.arange(ROPE // 2, dtype=jnp.float32) / ROPE)
    angles = positions[:, None] * frequency[None, :]
    cos_val = jnp.cos(angles)
    sin_val = jnp.sin(angles)
    queries = jnp.dot(normed, w_query, preferred_element_type=jnp.float32).reshape(
        row_count, heads_local, NOPE + ROPE
    )
    q_nope = queries[:, :, :NOPE].astype(jnp.bfloat16)
    q_rope = rotate(queries[:, :, NOPE:], cos_val[:, None, :], sin_val[:, None, :]).astype(
        jnp.bfloat16
    )
    kv_part = jnp.dot(normed, w_latent, preferred_element_type=jnp.float32)
    kv_all = lax.all_gather(kv_part, "tp", axis=1, tiled=True)
    kv_all, down_late, out_late = lax.optimization_barrier((kv_all, w_down, w_out))
    new_lat = kv_all[:, :LATENT] * rms_scale(kv_all[:, :LATENT]) * kv_gain
    new_rope = rotate(kv_all[:, LATENT:], cos_val, sin_val)
    new_keys = jnp.concatenate([new_lat, new_rope], axis=1).astype(jnp.bfloat16)
    key_up = w_key_up.reshape(LATENT, heads_local, NOPE)
    q_lat = jnp.einsum("nhc,lhc->nhl", q_nope, key_up, preferred_element_type=jnp.float32).astype(
        jnp.bfloat16
    )
    query_key = jnp.concatenate([q_lat, q_rope], axis=2)
    cache_keys = latent_cache.reshape(req_local, max_len, LATENT + ROPE)
    page_hot = page_table[:, :, None] == jnp.arange(PAGES, dtype=jnp.int32)[None, None, :]
    logical_page = jnp.sum(
        jnp.where(page_hot, jnp.arange(PAGES, dtype=jnp.int32)[None, :, None], 0), axis=1
    )
    logical_pos = (
        logical_page[:, :, None] * PAGE + jnp.arange(PAGE, dtype=jnp.int32)[None, None, :]
    ).reshape(req_local, max_len)
    live_mask = logical_pos < cache_len[:, None]
    score_scale = (NOPE + ROPE) ** (-0.5)
    grouped = query_key.reshape(req_local, STEPS * BEAMS * heads_local, LATENT + ROPE)
    s_cache = (
        jnp.einsum("rqd,rld->rql", grouped, cache_keys, preferred_element_type=jnp.float32)
        * score_scale
    )
    s_cache = jnp.where(live_mask[:, None, :], s_cache, -jnp.inf).reshape(
        req_local, STEPS, BEAMS, heads_local, max_len
    )
    fresh = new_keys.reshape(req_local, STEPS, BEAMS, LATENT + ROPE)
    beam_ids = jnp.arange(BEAMS, dtype=jnp.int32)
    lineage_rows = []
    for step_index in range(STEPS):
        lineage = jnp.broadcast_to(beam_ids[None, :], (req_local, BEAMS))
        pieces = [None] * STEPS
        for earlier in range(step_index, -1, -1):
            pieces[earlier] = lineage
            if earlier > 0:
                lineage_hot = lineage[:, :, None] == beam_ids[None, None, :]
                lineage = jnp.sum(
                    jnp.where(lineage_hot, parents[:, earlier - 1][:, None, :], 0), axis=2
                )
        for later in range(step_index + 1, STEPS):
            pieces[later] = jnp.full((req_local, BEAMS), -1, jnp.int32)
        lineage_rows.append(jnp.stack(pieces, axis=2))
    lineage_all = jnp.stack(lineage_rows, axis=1)
    pick = (lineage_all[..., None] == beam_ids).astype(jnp.bfloat16)
    tail_keys = jnp.einsum(
        "rsbja,rjad->rsbjd", pick, fresh, preferred_element_type=jnp.float32
    ).astype(jnp.bfloat16)
    queries_tail = query_key.reshape(req_local, STEPS, BEAMS, heads_local, LATENT + ROPE)
    s_tail = (
        jnp.einsum(
            "rsbhd,rsbjd->rsbhj", queries_tail, tail_keys, preferred_element_type=jnp.float32
        )
        * score_scale
    )
    causal = jnp.arange(STEPS)[None, :] <= jnp.arange(STEPS)[:, None]
    s_tail = jnp.where(causal[None, :, None, None, :], s_tail, -jnp.inf)
    top_score = jnp.maximum(jnp.max(s_cache, axis=-1), jnp.max(s_tail, axis=-1))
    e_cache = jnp.exp(s_cache - top_score[..., None])
    e_tail = jnp.exp(s_tail - top_score[..., None])
    total = jnp.sum(e_cache, axis=-1) + jnp.sum(e_tail, axis=-1)
    p_cache = (e_cache / total[..., None]).astype(jnp.bfloat16)
    p_tail = (e_tail / total[..., None]).astype(jnp.bfloat16)
    context = jnp.einsum(
        "rsbhl,rld->rsbhd", p_cache, cache_keys[..., :LATENT], preferred_element_type=jnp.float32
    )
    context = context + jnp.einsum(
        "rsbhj,rsbjd->rsbhd", p_tail, tail_keys[..., :LATENT], preferred_element_type=jnp.float32
    )
    context = context.astype(jnp.bfloat16).reshape(row_count, heads_local, LATENT)
    value_up = w_value_up.reshape(LATENT, heads_local, VDIM)
    head_out = (
        jnp.einsum("nhl,lhv->nhv", context, value_up, preferred_element_type=jnp.float32)
        .astype(jnp.bfloat16)
        .reshape(row_count, heads_local * VDIM)
    )
    expert_count = EXP_DEV * req_count
    capacity = min(row_count, 2 * row_count * TOPK // expert_count)
    slot_count = expert_count * capacity
    picks = routes.reshape(-1)
    pick_hot = (picks[:, None] == jnp.arange(expert_count, dtype=jnp.int32)[None, :]).astype(
        jnp.int32
    )
    before = jnp.cumsum(pick_hot, axis=0) - pick_hot
    ranks = jnp.sum(before * pick_hot, axis=1)
    slot_of = picks * capacity + ranks
    slot_hot = (slot_of[:, None] == jnp.arange(slot_count, dtype=jnp.int32)[None, :]).reshape(
        row_count, TOPK, slot_count
    )
    gather_rows = jnp.sum(slot_hot.astype(jnp.int32), axis=1).astype(jnp.bfloat16)
    weight_rows = jnp.sum(jnp.where(slot_hot, route_weights[:, :, None], 0.0), axis=1)
    tp_index = lax.axis_index("tp")
    col_start = tp_index * col_share
    head_all = lax.all_gather(head_out, "tp", axis=1, tiled=True)
    head_all, down_cols, out_cols = lax.optimization_barrier(
        (head_all, by_columns(down_late), by_columns(out_late))
    )
    attn_cols = jnp.dot(
        head_all, out_cols.reshape(-1, col_share), preferred_element_type=jnp.float32
    )
    hidden_cols = lax.dynamic_slice_in_dim(hidden_f, col_start, col_share, 1)
    resid_cols = hidden_cols + attn_cols
    square_sum = lax.psum(jnp.sum(resid_cols * resid_cols, axis=-1, keepdims=True), "tp")
    moe_scale = lax.rsqrt(square_sum / D + eps)
    gain_cols = lax.dynamic_slice_in_dim(moe_gain, col_start, col_share, 0)
    moe_in_cols = (resid_cols * moe_scale * gain_cols).astype(jnp.bfloat16)
    placed = jnp.dot(gather_rows.T, moe_in_cols, preferred_element_type=jnp.float32).astype(
        jnp.bfloat16
    )
    arrived_cols = lax.all_to_all(
        placed.reshape(req_count, EXP_DEV, capacity, col_share),
        "req",
        split_axis=0,
        concat_axis=0,
        tiled=True,
    )
    arrived = lax.all_gather(arrived_cols, "tp", axis=3, tiled=True)
    shares = expert_math(arrived, w_gate, w_up, down_cols)
    returned = send_home(shares)
    combined = jnp.dot(
        weight_rows, returned.reshape(slot_count, col_share).astype(jnp.float32), precision=highest
    )
    return (resid_cols + combined).astype(jnp.bfloat16)


def solution(mesh):
    in_specs = (
        P("req", None),
        P(),
        P(None, "tp"),
        P(None, "tp"),
        P(),
        P(None, "tp"),
        P(None, "tp"),
        P("tp", None),
        P(),
        P("req", None, "tp"),
        P("req", None, "tp"),
        P("req", "tp", None),
        P("req", None, None),
        P("req", None),
        P("req"),
        P("req", None, None),
        P("req", None),
        P("req", None),
    )
    out_specs = P("req", "tp")
    return jax.shard_map(local, mesh=mesh, in_specs=in_specs, out_specs=out_specs, check_vma=False)
```

```python
import jax
import jax.numpy as jnp
from jax import lax
from jax.sharding import PartitionSpec as P

D = 2048
NOPE = 128
ROPE = 64
VDIM = 128
LATENT = 512
TOPK = 6
EXP_DEV = 1
BEAMS = 8
STEPS = 4
PAGE = 64
PAGES = 8


eps = 1e-06
rope_base = 50000.0


def rms_scale(values):
    return lax.rsqrt(jnp.mean(values * values, axis=-1, keepdims=True) + eps)


def rotate(values, cos_val, sin_val):
    half_rope = values.shape[-1] // 2
    first = values[..., :half_rope]
    second = values[..., half_rope:]
    return jnp.concatenate(
        [first * cos_val - second * sin_val, second * cos_val + first * sin_val], axis=-1
    )


def expert_math(arrived, gate_w, up_w, down_pieces):
    gate_val = jnp.einsum("nesd,edf->nesf", arrived, gate_w, preferred_element_type=jnp.float32)
    up_val = jnp.einsum("nesd,edf->nesf", arrived, up_w, preferred_element_type=jnp.float32)
    active = (jax.nn.silu(gate_val) * up_val).astype(jnp.bfloat16)
    active_all = lax.all_gather(active, "tp", axis=0)
    tp_count = lax.axis_size("tp")
    tp_index = lax.axis_index("tp")
    total = None
    for shift in range(tp_count):
        source = lax.dynamic_index_in_dim(
            active_all, (tp_index - shift) % tp_count, 0, keepdims=False
        )
        term = jnp.einsum(
            "nesf,efd->nesd", source, down_pieces[shift], preferred_element_type=jnp.float32
        )
        total = term if total is None else total + term
    return total.astype(jnp.bfloat16)


def by_columns(weight):
    tp_count = lax.axis_size("tp")
    tp_index = lax.axis_index("tp")
    col_share = weight.shape[-1] // tp_count
    pieces = [None] * tp_count
    for shift in range(tp_count):
        target = (tp_index + shift) % tp_count
        piece = lax.dynamic_slice_in_dim(weight, target * col_share, col_share, weight.ndim - 1)
        if shift:
            piece = lax.ppermute(
                piece, "tp", [(s, (s + shift) % tp_count) for s in range(tp_count)]
            )
        pieces[shift] = piece
    return pieces


def send_home(shares):
    return lax.all_to_all(shares, "req", split_axis=0, concat_axis=0, tiled=True)


def local(
    hidden_in,
    attn_gain,
    w_query,
    w_latent,
    kv_gain,
    w_key_up,
    w_value_up,
    w_out,
    moe_gain,
    w_gate,
    w_up,
    w_down,
    latent_cache,
    page_table,
    cache_len,
    parents,
    routes,
    route_weights,
):
    highest = lax.Precision.HIGHEST
    row_count = hidden_in.shape[0]
    req_local = cache_len.shape[0]
    heads_local = w_value_up.shape[1] // VDIM
    tp_count = lax.axis_size("tp")
    req_count = lax.axis_size("req")
    col_share = D // tp_count
    max_len = PAGES * PAGE
    hidden_f = hidden_in.astype(jnp.float32)
    normed = (hidden_f * rms_scale(hidden_f) * attn_gain).astype(jnp.bfloat16)
    positions = (
        cache_len.astype(jnp.float32)[:, None, None]
        + jnp.arange(STEPS, dtype=jnp.float32)[None, :, None]
        + jnp.zeros((1, 1, BEAMS), jnp.float32)
    ).reshape(row_count)
    frequency = rope_base ** (-2.0 * jnp.arange(ROPE // 2, dtype=jnp.float32) / ROPE)
    angles = positions[:, None] * frequency[None, :]
    cos_val = jnp.cos(angles)
    sin_val = jnp.sin(angles)
    queries = jnp.dot(normed, w_query, preferred_element_type=jnp.float32).reshape(
        row_count, heads_local, NOPE + ROPE
    )
    q_nope = queries[:, :, :NOPE].astype(jnp.bfloat16)
    q_rope = rotate(queries[:, :, NOPE:], cos_val[:, None, :], sin_val[:, None, :]).astype(
        jnp.bfloat16
    )
    kv_part = jnp.dot(normed, w_latent, preferred_element_type=jnp.float32)
    kv_all = lax.all_gather(kv_part, "tp", axis=1, tiled=True)
    kv_all, down_late, out_late = lax.optimization_barrier((kv_all, w_down, w_out))
    new_lat = kv_all[:, :LATENT] * rms_scale(kv_all[:, :LATENT]) * kv_gain
    new_rope = rotate(kv_all[:, LATENT:], cos_val, sin_val)
    new_keys = jnp.concatenate([new_lat, new_rope], axis=1).astype(jnp.bfloat16)
    key_up = w_key_up.reshape(LATENT, heads_local, NOPE)
    q_lat = jnp.einsum("nhc,lhc->nhl", q_nope, key_up, preferred_element_type=jnp.float32).astype(
        jnp.bfloat16
    )
    query_key = jnp.concatenate([q_lat, q_rope], axis=2)
    cache_keys = latent_cache.reshape(req_local, max_len, LATENT + ROPE)
    page_hot = page_table[:, :, None] == jnp.arange(PAGES, dtype=jnp.int32)[None, None, :]
    logical_page = jnp.sum(
        jnp.where(page_hot, jnp.arange(PAGES, dtype=jnp.int32)[None, :, None], 0), axis=1
    )
    logical_pos = (
        logical_page[:, :, None] * PAGE + jnp.arange(PAGE, dtype=jnp.int32)[None, None, :]
    ).reshape(req_local, max_len)
    live_mask = logical_pos < cache_len[:, None]
    score_scale = (NOPE + ROPE) ** (-0.5)
    grouped = query_key.reshape(req_local, STEPS * BEAMS * heads_local, LATENT + ROPE)
    s_cache = (
        jnp.einsum("rqd,rld->rql", grouped, cache_keys, preferred_element_type=jnp.float32)
        * score_scale
    )
    s_cache = jnp.where(live_mask[:, None, :], s_cache, -jnp.inf).reshape(
        req_local, STEPS, BEAMS, heads_local, max_len
    )
    fresh = new_keys.reshape(req_local, STEPS, BEAMS, LATENT + ROPE)
    beam_ids = jnp.arange(BEAMS, dtype=jnp.int32)
    lineage_rows = []
    for step_index in range(STEPS):
        lineage = jnp.broadcast_to(beam_ids[None, :], (req_local, BEAMS))
        pieces = [None] * STEPS
        for earlier in range(step_index, -1, -1):
            pieces[earlier] = lineage
            if earlier > 0:
                lineage_hot = lineage[:, :, None] == beam_ids[None, None, :]
                lineage = jnp.sum(
                    jnp.where(lineage_hot, parents[:, earlier - 1][:, None, :], 0), axis=2
                )
        for later in range(step_index + 1, STEPS):
            pieces[later] = jnp.full((req_local, BEAMS), -1, jnp.int32)
        lineage_rows.append(jnp.stack(pieces, axis=2))
    lineage_all = jnp.stack(lineage_rows, axis=1)
    pick = (lineage_all[..., None] == beam_ids).astype(jnp.bfloat16)
    tail_keys = jnp.einsum(
        "rsbja,rjad->rsbjd", pick, fresh, preferred_element_type=jnp.float32
    ).astype(jnp.bfloat16)
    queries_tail = query_key.reshape(req_local, STEPS, BEAMS, heads_local, LATENT + ROPE)
    s_tail = (
        jnp.einsum(
            "rsbhd,rsbjd->rsbhj", queries_tail, tail_keys, preferred_element_type=jnp.float32
        )
        * score_scale
    )
    causal = jnp.arange(STEPS)[None, :] <= jnp.arange(STEPS)[:, None]
    s_tail = jnp.where(causal[None, :, None, None, :], s_tail, -jnp.inf)
    top_score = jnp.maximum(jnp.max(s_cache, axis=-1), jnp.max(s_tail, axis=-1))
    e_cache = jnp.exp(s_cache - top_score[..., None])
    e_tail = jnp.exp(s_tail - top_score[..., None])
    total = jnp.sum(e_cache, axis=-1) + jnp.sum(e_tail, axis=-1)
    p_cache = (e_cache / total[..., None]).astype(jnp.bfloat16)
    p_tail = (e_tail / total[..., None]).astype(jnp.bfloat16)
    context = jnp.einsum(
        "rsbhl,rld->rsbhd", p_cache, cache_keys[..., :LATENT], preferred_element_type=jnp.float32
    )
    context = context + jnp.einsum(
        "rsbhj,rsbjd->rsbhd", p_tail, tail_keys[..., :LATENT], preferred_element_type=jnp.float32
    )
    context = context.astype(jnp.bfloat16).reshape(row_count, heads_local, LATENT)
    value_up = w_value_up.reshape(LATENT, heads_local, VDIM)
    head_out = (
        jnp.einsum("nhl,lhv->nhv", context, value_up, preferred_element_type=jnp.float32)
        .astype(jnp.bfloat16)
        .reshape(row_count, heads_local * VDIM)
    )
    expert_count = EXP_DEV * req_count
    capacity = min(row_count, 2 * row_count * TOPK // expert_count)
    slot_count = expert_count * capacity
    picks = routes.reshape(-1)
    pick_hot = (picks[:, None] == jnp.arange(expert_count, dtype=jnp.int32)[None, :]).astype(
        jnp.int32
    )
    before = jnp.cumsum(pick_hot, axis=0) - pick_hot
    ranks = jnp.sum(before * pick_hot, axis=1)
    slot_of = picks * capacity + ranks
    slot_hot = (slot_of[:, None] == jnp.arange(slot_count, dtype=jnp.int32)[None, :]).reshape(
        row_count, TOPK, slot_count
    )
    gather_rows = jnp.sum(slot_hot.astype(jnp.int32), axis=1).astype(jnp.bfloat16)
    weight_rows = jnp.sum(jnp.where(slot_hot, route_weights[:, :, None], 0.0), axis=1)
    tp_index = lax.axis_index("tp")
    col_start = tp_index * col_share
    head_all = lax.all_gather(head_out, "tp", axis=1, tiled=True)
    head_all, down_pieces, out_pieces = lax.optimization_barrier(
        (head_all, by_columns(down_late), by_columns(out_late))
    )
    head_blocks = [
        head_all[:, block * col_share : (block + 1) * col_share] for block in range(tp_count)
    ]
    head_doubled = jnp.concatenate(head_blocks[::-1] + head_blocks[::-1], axis=1)
    head_shift = lax.dynamic_slice_in_dim(
        head_doubled, (tp_count - 1 - tp_index) * col_share, tp_count * col_share, 1
    )
    attn_cols = jnp.dot(
        head_shift, jnp.concatenate(out_pieces, axis=0), preferred_element_type=jnp.float32
    )
    hidden_cols = lax.dynamic_slice_in_dim(hidden_f, col_start, col_share, 1)
    resid_cols = hidden_cols + attn_cols
    square_sum = lax.psum(jnp.sum(resid_cols * resid_cols, axis=-1, keepdims=True), "tp")
    moe_scale = lax.rsqrt(square_sum / D + eps)
    gain_cols = lax.dynamic_slice_in_dim(moe_gain, col_start, col_share, 0)
    moe_in_cols = (resid_cols * moe_scale * gain_cols).astype(jnp.bfloat16)
    placed = jnp.dot(gather_rows.T, moe_in_cols, preferred_element_type=jnp.float32).astype(
        jnp.bfloat16
    )
    arrived_cols = lax.all_to_all(
        placed.reshape(req_count, EXP_DEV, capacity, col_share),
        "req",
        split_axis=0,
        concat_axis=0,
        tiled=True,
    )
    arrived = lax.all_gather(arrived_cols, "tp", axis=3, tiled=True)
    shares = expert_math(arrived, w_gate, w_up, down_pieces)
    returned = send_home(shares)
    combined = jnp.dot(
        weight_rows, returned.reshape(slot_count, col_share).astype(jnp.float32), precision=highest
    )
    return (resid_cols + combined).astype(jnp.bfloat16)


def solution(mesh):
    in_specs = (
        P("req", None),
        P(),
        P(None, "tp"),
        P(None, "tp"),
        P(),
        P(None, "tp"),
        P(None, "tp"),
        P("tp", None),
        P(),
        P("req", None, "tp"),
        P("req", None, "tp"),
        P("req", "tp", None),
        P("req", None, None),
        P("req", None),
        P("req"),
        P("req", None, None),
        P("req", None),
        P("req", None),
    )
    out_specs = P("req", "tp")
    return jax.shard_map(local, mesh=mesh, in_specs=in_specs, out_specs=out_specs, check_vma=False)
```

```python
import jax
import jax.numpy as jnp
from jax import lax
from jax.sharding import PartitionSpec as P

D = 2048
NOPE = 128
ROPE = 64
VDIM = 128
LATENT = 512
TOPK = 6
EXP_DEV = 1
BEAMS = 8
STEPS = 4
PAGE = 64
PAGES = 8


eps = 1e-06
rope_base = 50000.0


def rms_scale(values):
    return lax.rsqrt(jnp.mean(values * values, axis=-1, keepdims=True) + eps)


def rotate(values, cos_val, sin_val):
    half_rope = values.shape[-1] // 2
    first = values[..., :half_rope]
    second = values[..., half_rope:]
    return jnp.concatenate(
        [first * cos_val - second * sin_val, second * cos_val + first * sin_val], axis=-1
    )


def expert_math(arrived, gate_w, up_w, down_pieces):
    gate_val = jnp.einsum("nesd,edf->nesf", arrived, gate_w, preferred_element_type=jnp.float32)
    up_val = jnp.einsum("nesd,edf->nesf", arrived, up_w, preferred_element_type=jnp.float32)
    active = (jax.nn.silu(gate_val) * up_val).astype(jnp.bfloat16)
    active_all = lax.all_gather(active, "tp", axis=0)
    tp_count = lax.axis_size("tp")
    tp_index = lax.axis_index("tp")
    total = None
    for shift in range(tp_count):
        source = lax.dynamic_index_in_dim(
            active_all, (tp_index - shift) % tp_count, 0, keepdims=False
        )
        term = jnp.einsum(
            "nesf,efd->nesd", source, down_pieces[shift], preferred_element_type=jnp.float32
        )
        total = term if total is None else total + term
    return total.astype(jnp.bfloat16)


def tp_shifted(values):
    tp_count = lax.axis_size("tp")
    pieces = [values]
    for shift in range(1, tp_count):
        pieces.append(
            lax.ppermute(values, "tp", [(s, (s + shift) % tp_count) for s in range(tp_count)])
        )
    return pieces


def by_columns(weight):
    tp_count = lax.axis_size("tp")
    tp_index = lax.axis_index("tp")
    col_share = weight.shape[-1] // tp_count
    pieces = [None] * tp_count
    for shift in range(tp_count):
        target = (tp_index + shift) % tp_count
        piece = lax.dynamic_slice_in_dim(weight, target * col_share, col_share, weight.ndim - 1)
        if shift:
            piece = lax.ppermute(
                piece, "tp", [(s, (s + shift) % tp_count) for s in range(tp_count)]
            )
        pieces[shift] = piece
    return pieces


def send_home(shares):
    return lax.all_to_all(shares, "req", split_axis=0, concat_axis=0, tiled=True)


def local(
    hidden_in,
    attn_gain,
    w_query,
    w_latent,
    kv_gain,
    w_key_up,
    w_value_up,
    w_out,
    moe_gain,
    w_gate,
    w_up,
    w_down,
    latent_cache,
    page_table,
    cache_len,
    parents,
    routes,
    route_weights,
):
    highest = lax.Precision.HIGHEST
    row_count = hidden_in.shape[0]
    req_local = cache_len.shape[0]
    heads_local = w_value_up.shape[1] // VDIM
    tp_count = lax.axis_size("tp")
    req_count = lax.axis_size("req")
    col_share = D // tp_count
    max_len = PAGES * PAGE
    hidden_f = hidden_in.astype(jnp.float32)
    normed = (hidden_f * rms_scale(hidden_f) * attn_gain).astype(jnp.bfloat16)
    positions = (
        cache_len.astype(jnp.float32)[:, None, None]
        + jnp.arange(STEPS, dtype=jnp.float32)[None, :, None]
        + jnp.zeros((1, 1, BEAMS), jnp.float32)
    ).reshape(row_count)
    frequency = rope_base ** (-2.0 * jnp.arange(ROPE // 2, dtype=jnp.float32) / ROPE)
    angles = positions[:, None] * frequency[None, :]
    cos_val = jnp.cos(angles)
    sin_val = jnp.sin(angles)
    queries = jnp.dot(normed, w_query, preferred_element_type=jnp.float32).reshape(
        row_count, heads_local, NOPE + ROPE
    )
    q_nope = queries[:, :, :NOPE].astype(jnp.bfloat16)
    q_rope = rotate(queries[:, :, NOPE:], cos_val[:, None, :], sin_val[:, None, :]).astype(
        jnp.bfloat16
    )
    kv_part = jnp.dot(normed, w_latent, preferred_element_type=jnp.float32)
    kv_pieces = tp_shifted(kv_part)[::-1]
    kv_all = lax.dynamic_slice_in_dim(
        jnp.concatenate(kv_pieces + kv_pieces, axis=1),
        (tp_count - 1 - lax.axis_index("tp")) * kv_part.shape[1],
        tp_count * kv_part.shape[1],
        1,
    )
    kv_all, down_late, out_late = lax.optimization_barrier((kv_all, w_down, w_out))
    new_lat = kv_all[:, :LATENT] * rms_scale(kv_all[:, :LATENT]) * kv_gain
    new_rope = rotate(kv_all[:, LATENT:], cos_val, sin_val)
    new_keys = jnp.concatenate([new_lat, new_rope], axis=1).astype(jnp.bfloat16)
    key_up = w_key_up.reshape(LATENT, heads_local, NOPE)
    q_lat = jnp.einsum("nhc,lhc->nhl", q_nope, key_up, preferred_element_type=jnp.float32).astype(
        jnp.bfloat16
    )
    query_key = jnp.concatenate([q_lat, q_rope], axis=2)
    cache_keys = latent_cache.reshape(req_local, max_len, LATENT + ROPE)
    page_hot = page_table[:, :, None] == jnp.arange(PAGES, dtype=jnp.int32)[None, None, :]
    logical_page = jnp.sum(
        jnp.where(page_hot, jnp.arange(PAGES, dtype=jnp.int32)[None, :, None], 0), axis=1
    )
    logical_pos = (
        logical_page[:, :, None] * PAGE + jnp.arange(PAGE, dtype=jnp.int32)[None, None, :]
    ).reshape(req_local, max_len)
    live_mask = logical_pos < cache_len[:, None]
    score_scale = (NOPE + ROPE) ** (-0.5)
    grouped = query_key.reshape(req_local, STEPS * BEAMS * heads_local, LATENT + ROPE)
    s_cache = (
        jnp.einsum("rqd,rld->rql", grouped, cache_keys, preferred_element_type=jnp.float32)
        * score_scale
    )
    s_cache = jnp.where(live_mask[:, None, :], s_cache, -jnp.inf).reshape(
        req_local, STEPS, BEAMS, heads_local, max_len
    )
    fresh = new_keys.reshape(req_local, STEPS, BEAMS, LATENT + ROPE)
    beam_ids = jnp.arange(BEAMS, dtype=jnp.int32)
    lineage_rows = []
    for step_index in range(STEPS):
        lineage = jnp.broadcast_to(beam_ids[None, :], (req_local, BEAMS))
        pieces = [None] * STEPS
        for earlier in range(step_index, -1, -1):
            pieces[earlier] = lineage
            if earlier > 0:
                lineage_hot = lineage[:, :, None] == beam_ids[None, None, :]
                lineage = jnp.sum(
                    jnp.where(lineage_hot, parents[:, earlier - 1][:, None, :], 0), axis=2
                )
        for later in range(step_index + 1, STEPS):
            pieces[later] = jnp.full((req_local, BEAMS), -1, jnp.int32)
        lineage_rows.append(jnp.stack(pieces, axis=2))
    lineage_all = jnp.stack(lineage_rows, axis=1)
    pick = (lineage_all[..., None] == beam_ids).astype(jnp.bfloat16)
    tail_keys = jnp.einsum(
        "rsbja,rjad->rsbjd", pick, fresh, preferred_element_type=jnp.float32
    ).astype(jnp.bfloat16)
    queries_tail = query_key.reshape(req_local, STEPS, BEAMS, heads_local, LATENT + ROPE)
    s_tail = (
        jnp.einsum(
            "rsbhd,rsbjd->rsbhj", queries_tail, tail_keys, preferred_element_type=jnp.float32
        )
        * score_scale
    )
    causal = jnp.arange(STEPS)[None, :] <= jnp.arange(STEPS)[:, None]
    s_tail = jnp.where(causal[None, :, None, None, :], s_tail, -jnp.inf)
    top_score = jnp.maximum(jnp.max(s_cache, axis=-1), jnp.max(s_tail, axis=-1))
    e_cache = jnp.exp(s_cache - top_score[..., None])
    e_tail = jnp.exp(s_tail - top_score[..., None])
    total = jnp.sum(e_cache, axis=-1) + jnp.sum(e_tail, axis=-1)
    p_cache = (e_cache / total[..., None]).astype(jnp.bfloat16)
    p_tail = (e_tail / total[..., None]).astype(jnp.bfloat16)
    context = jnp.einsum(
        "rsbhl,rld->rsbhd", p_cache, cache_keys[..., :LATENT], preferred_element_type=jnp.float32
    )
    context = context + jnp.einsum(
        "rsbhj,rsbjd->rsbhd", p_tail, tail_keys[..., :LATENT], preferred_element_type=jnp.float32
    )
    context = context.astype(jnp.bfloat16).reshape(row_count, heads_local, LATENT)
    value_up = w_value_up.reshape(LATENT, heads_local, VDIM)
    head_out = (
        jnp.einsum("nhl,lhv->nhv", context, value_up, preferred_element_type=jnp.float32)
        .astype(jnp.bfloat16)
        .reshape(row_count, heads_local * VDIM)
    )
    expert_count = EXP_DEV * req_count
    capacity = min(row_count, 2 * row_count * TOPK // expert_count)
    slot_count = expert_count * capacity
    picks = routes.reshape(-1)
    pick_hot = (picks[:, None] == jnp.arange(expert_count, dtype=jnp.int32)[None, :]).astype(
        jnp.int32
    )
    before = jnp.cumsum(pick_hot, axis=0) - pick_hot
    ranks = jnp.sum(before * pick_hot, axis=1)
    slot_of = picks * capacity + ranks
    slot_hot = (slot_of[:, None] == jnp.arange(slot_count, dtype=jnp.int32)[None, :]).reshape(
        row_count, TOPK, slot_count
    )
    gather_rows = jnp.sum(slot_hot.astype(jnp.int32), axis=1).astype(jnp.bfloat16)
    weight_rows = jnp.sum(jnp.where(slot_hot, route_weights[:, :, None], 0.0), axis=1)
    tp_index = lax.axis_index("tp")
    col_start = tp_index * col_share
    head_shift = jnp.concatenate(tp_shifted(head_out), axis=1)
    head_shift, down_pieces, out_pieces = lax.optimization_barrier(
        (head_shift, by_columns(down_late), by_columns(out_late))
    )
    attn_cols = jnp.dot(
        head_shift, jnp.concatenate(out_pieces, axis=0), preferred_element_type=jnp.float32
    )
    hidden_cols = lax.dynamic_slice_in_dim(hidden_f, col_start, col_share, 1)
    resid_cols = hidden_cols + attn_cols
    square_sum = sum(tp_shifted(jnp.sum(resid_cols * resid_cols, axis=-1, keepdims=True)))
    moe_scale = lax.rsqrt(square_sum / D + eps)
    gain_cols = lax.dynamic_slice_in_dim(moe_gain, col_start, col_share, 0)
    moe_in_cols = (resid_cols * moe_scale * gain_cols).astype(jnp.bfloat16)
    placed = jnp.dot(gather_rows.T, moe_in_cols, preferred_element_type=jnp.float32).astype(
        jnp.bfloat16
    )
    arrived_cols = lax.all_to_all(
        placed.reshape(req_count, EXP_DEV, capacity, col_share),
        "req",
        split_axis=0,
        concat_axis=0,
        tiled=True,
    )
    arrived = lax.all_gather(arrived_cols, "tp", axis=3, tiled=True)
    shares = expert_math(arrived, w_gate, w_up, down_pieces)
    returned = send_home(shares)
    combined = jnp.dot(
        weight_rows, returned.reshape(slot_count, col_share).astype(jnp.float32), precision=highest
    )
    return (resid_cols + combined).astype(jnp.bfloat16)


def solution(mesh):
    in_specs = (
        P("req", None),
        P(),
        P(None, "tp"),
        P(None, "tp"),
        P(),
        P(None, "tp"),
        P(None, "tp"),
        P("tp", None),
        P(),
        P("req", None, "tp"),
        P("req", None, "tp"),
        P("req", "tp", None),
        P("req", None, None),
        P("req", None),
        P("req"),
        P("req", None, None),
        P("req", None),
        P("req", None),
    )
    out_specs = P("req", "tp")
    return jax.shard_map(local, mesh=mesh, in_specs=in_specs, out_specs=out_specs, check_vma=False)
```

```python
import jax
import jax.numpy as jnp
from jax import lax
from jax.sharding import PartitionSpec as P

D = 2048
NOPE = 128
ROPE = 64
VDIM = 128
LATENT = 512
TOPK = 6
EXP_DEV = 1
BEAMS = 8
STEPS = 4
PAGE = 64
PAGES = 8


eps = 1e-06
rope_base = 50000.0


def rms_scale(values):
    return lax.rsqrt(jnp.mean(values * values, axis=-1, keepdims=True) + eps)


def rotate(values, cos_val, sin_val):
    half_rope = values.shape[-1] // 2
    first = values[..., :half_rope]
    second = values[..., half_rope:]
    return jnp.concatenate(
        [first * cos_val - second * sin_val, second * cos_val + first * sin_val], axis=-1
    )


def expert_math(arrived, gate_w, up_w, down_pieces):
    gate_val = jnp.einsum("nesd,edf->nesf", arrived, gate_w, preferred_element_type=jnp.float32)
    up_val = jnp.einsum("nesd,edf->nesf", arrived, up_w, preferred_element_type=jnp.float32)
    active = (jax.nn.silu(gate_val) * up_val).astype(jnp.bfloat16)
    active_all = lax.all_gather(active, "tp", axis=0)
    tp_count = lax.axis_size("tp")
    tp_index = lax.axis_index("tp")
    total = None
    for shift in range(tp_count):
        source = lax.dynamic_index_in_dim(
            active_all, (tp_index - shift) % tp_count, 0, keepdims=False
        )
        term = jnp.einsum(
            "nesf,efd->nesd", source, down_pieces[shift], preferred_element_type=jnp.float32
        )
        total = term if total is None else total + term
    return total.astype(jnp.bfloat16)


def tp_shifted(values):
    tp_count = lax.axis_size("tp")
    pieces = [values]
    for shift in range(1, tp_count):
        pieces.append(
            lax.ppermute(values, "tp", [(s, (s + shift) % tp_count) for s in range(tp_count)])
        )
    return pieces


def by_columns(down_w, out_w):
    tp_count = lax.axis_size("tp")
    tp_index = lax.axis_index("tp")
    col_share = out_w.shape[-1] // tp_count
    down_rows = down_w.shape[1]
    down_pieces, out_pieces = [], []
    for shift in range(tp_count):
        start = ((tp_index + shift) % tp_count) * col_share
        piece = jnp.concatenate(
            [
                lax.dynamic_slice_in_dim(down_w[0], start, col_share, 1),
                lax.dynamic_slice_in_dim(out_w, start, col_share, 1),
            ],
            axis=0,
        )
        if shift:
            piece = lax.ppermute(
                piece, "tp", [(s, (s + shift) % tp_count) for s in range(tp_count)]
            )
        down_pieces.append(piece[None, :down_rows])
        out_pieces.append(piece[down_rows:])
    return down_pieces, out_pieces


def send_home(shares):
    return lax.all_to_all(shares, "req", split_axis=0, concat_axis=0, tiled=True)


def local(
    hidden_in,
    attn_gain,
    w_query,
    w_latent,
    kv_gain,
    w_key_up,
    w_value_up,
    w_out,
    moe_gain,
    w_gate,
    w_up,
    w_down,
    latent_cache,
    page_table,
    cache_len,
    parents,
    routes,
    route_weights,
):
    highest = lax.Precision.HIGHEST
    row_count = hidden_in.shape[0]
    req_local = cache_len.shape[0]
    heads_local = w_value_up.shape[1] // VDIM
    tp_count = lax.axis_size("tp")
    req_count = lax.axis_size("req")
    col_share = D // tp_count
    max_len = PAGES * PAGE
    hidden_f = hidden_in.astype(jnp.float32)
    normed = (hidden_f * rms_scale(hidden_f) * attn_gain).astype(jnp.bfloat16)
    normed, down_late, out_late = lax.optimization_barrier((normed, w_down, w_out))
    positions = (
        cache_len.astype(jnp.float32)[:, None, None]
        + jnp.arange(STEPS, dtype=jnp.float32)[None, :, None]
        + jnp.zeros((1, 1, BEAMS), jnp.float32)
    ).reshape(row_count)
    frequency = rope_base ** (-2.0 * jnp.arange(ROPE // 2, dtype=jnp.float32) / ROPE)
    angles = positions[:, None] * frequency[None, :]
    cos_val = jnp.cos(angles)
    sin_val = jnp.sin(angles)
    queries = jnp.dot(normed, w_query, preferred_element_type=jnp.float32).reshape(
        row_count, heads_local, NOPE + ROPE
    )
    q_nope = queries[:, :, :NOPE].astype(jnp.bfloat16)
    q_rope = rotate(queries[:, :, NOPE:], cos_val[:, None, :], sin_val[:, None, :]).astype(
        jnp.bfloat16
    )
    kv_part = jnp.dot(normed, w_latent, preferred_element_type=jnp.float32)
    kv_pieces = tp_shifted(kv_part)[::-1]
    kv_all = lax.dynamic_slice_in_dim(
        jnp.concatenate(kv_pieces + kv_pieces, axis=1),
        (tp_count - 1 - lax.axis_index("tp")) * kv_part.shape[1],
        tp_count * kv_part.shape[1],
        1,
    )
    new_lat = kv_all[:, :LATENT] * rms_scale(kv_all[:, :LATENT]) * kv_gain
    new_rope = rotate(kv_all[:, LATENT:], cos_val, sin_val)
    new_keys = jnp.concatenate([new_lat, new_rope], axis=1).astype(jnp.bfloat16)
    key_up = w_key_up.reshape(LATENT, heads_local, NOPE)
    q_lat = jnp.einsum("nhc,lhc->nhl", q_nope, key_up, preferred_element_type=jnp.float32).astype(
        jnp.bfloat16
    )
    query_key = jnp.concatenate([q_lat, q_rope], axis=2)
    cache_keys = latent_cache.reshape(req_local, max_len, LATENT + ROPE)
    page_hot = page_table[:, :, None] == jnp.arange(PAGES, dtype=jnp.int32)[None, None, :]
    logical_page = jnp.sum(
        jnp.where(page_hot, jnp.arange(PAGES, dtype=jnp.int32)[None, :, None], 0), axis=1
    )
    logical_pos = (
        logical_page[:, :, None] * PAGE + jnp.arange(PAGE, dtype=jnp.int32)[None, None, :]
    ).reshape(req_local, max_len)
    live_mask = logical_pos < cache_len[:, None]
    score_scale = (NOPE + ROPE) ** (-0.5)
    grouped = query_key.reshape(req_local, STEPS * BEAMS * heads_local, LATENT + ROPE)
    s_cache = (
        jnp.einsum("rqd,rld->rql", grouped, cache_keys, preferred_element_type=jnp.float32)
        * score_scale
    )
    s_cache = jnp.where(live_mask[:, None, :], s_cache, -jnp.inf).reshape(
        req_local, STEPS, BEAMS, heads_local, max_len
    )
    fresh = new_keys.reshape(req_local, STEPS, BEAMS, LATENT + ROPE)
    beam_ids = jnp.arange(BEAMS, dtype=jnp.int32)
    lineage_rows = []
    for step_index in range(STEPS):
        lineage = jnp.broadcast_to(beam_ids[None, :], (req_local, BEAMS))
        pieces = [None] * STEPS
        for earlier in range(step_index, -1, -1):
            pieces[earlier] = lineage
            if earlier > 0:
                lineage_hot = lineage[:, :, None] == beam_ids[None, None, :]
                lineage = jnp.sum(
                    jnp.where(lineage_hot, parents[:, earlier - 1][:, None, :], 0), axis=2
                )
        for later in range(step_index + 1, STEPS):
            pieces[later] = jnp.full((req_local, BEAMS), -1, jnp.int32)
        lineage_rows.append(jnp.stack(pieces, axis=2))
    lineage_all = jnp.stack(lineage_rows, axis=1)
    pick = (lineage_all[..., None] == beam_ids).astype(jnp.bfloat16)
    tail_keys = jnp.einsum(
        "rsbja,rjad->rsbjd", pick, fresh, preferred_element_type=jnp.float32
    ).astype(jnp.bfloat16)
    queries_tail = query_key.reshape(req_local, STEPS, BEAMS, heads_local, LATENT + ROPE)
    s_tail = (
        jnp.einsum(
            "rsbhd,rsbjd->rsbhj", queries_tail, tail_keys, preferred_element_type=jnp.float32
        )
        * score_scale
    )
    causal = jnp.arange(STEPS)[None, :] <= jnp.arange(STEPS)[:, None]
    s_tail = jnp.where(causal[None, :, None, None, :], s_tail, -jnp.inf)
    top_score = jnp.maximum(jnp.max(s_cache, axis=-1), jnp.max(s_tail, axis=-1))
    e_cache = jnp.exp(s_cache - top_score[..., None])
    e_tail = jnp.exp(s_tail - top_score[..., None])
    total = jnp.sum(e_cache, axis=-1) + jnp.sum(e_tail, axis=-1)
    p_cache = (e_cache / total[..., None]).astype(jnp.bfloat16)
    p_tail = (e_tail / total[..., None]).astype(jnp.bfloat16)
    context = jnp.einsum(
        "rsbhl,rld->rsbhd", p_cache, cache_keys[..., :LATENT], preferred_element_type=jnp.float32
    )
    context = context + jnp.einsum(
        "rsbhj,rsbjd->rsbhd", p_tail, tail_keys[..., :LATENT], preferred_element_type=jnp.float32
    )
    context = context.astype(jnp.bfloat16).reshape(row_count, heads_local, LATENT)
    value_up = w_value_up.reshape(LATENT, heads_local, VDIM)
    head_out = (
        jnp.einsum("nhl,lhv->nhv", context, value_up, preferred_element_type=jnp.float32)
        .astype(jnp.bfloat16)
        .reshape(row_count, heads_local * VDIM)
    )
    expert_count = EXP_DEV * req_count
    capacity = min(row_count, 2 * row_count * TOPK // expert_count)
    slot_count = expert_count * capacity
    picks = routes.reshape(-1)
    pick_hot = (picks[:, None] == jnp.arange(expert_count, dtype=jnp.int32)[None, :]).astype(
        jnp.int32
    )
    before = jnp.cumsum(pick_hot, axis=0) - pick_hot
    ranks = jnp.sum(before * pick_hot, axis=1)
    slot_of = picks * capacity + ranks
    slot_hot = (slot_of[:, None] == jnp.arange(slot_count, dtype=jnp.int32)[None, :]).reshape(
        row_count, TOPK, slot_count
    )
    gather_rows = jnp.sum(slot_hot.astype(jnp.int32), axis=1).astype(jnp.bfloat16)
    weight_rows = jnp.sum(jnp.where(slot_hot, route_weights[:, :, None], 0.0), axis=1)
    tp_index = lax.axis_index("tp")
    col_start = tp_index * col_share
    head_shift = jnp.concatenate(tp_shifted(head_out), axis=1)
    head_shift, down_pieces, out_pieces = lax.optimization_barrier(
        (head_shift,) + by_columns(down_late, out_late)
    )
    attn_cols = jnp.dot(
        head_shift, jnp.concatenate(out_pieces, axis=0), preferred_element_type=jnp.float32
    )
    hidden_cols = lax.dynamic_slice_in_dim(hidden_f, col_start, col_share, 1)
    resid_cols = hidden_cols + attn_cols
    square_sum = sum(tp_shifted(jnp.sum(resid_cols * resid_cols, axis=-1, keepdims=True)))
    moe_scale = lax.rsqrt(square_sum / D + eps)
    gain_cols = lax.dynamic_slice_in_dim(moe_gain, col_start, col_share, 0)
    moe_in_cols = (resid_cols * moe_scale * gain_cols).astype(jnp.bfloat16)
    placed = jnp.dot(gather_rows.T, moe_in_cols, preferred_element_type=jnp.float32).astype(
        jnp.bfloat16
    )
    arrived_cols = lax.all_to_all(
        placed.reshape(req_count, EXP_DEV, capacity, col_share),
        "req",
        split_axis=0,
        concat_axis=0,
        tiled=True,
    )
    arrived = lax.all_gather(arrived_cols, "tp", axis=3, tiled=True)
    shares = expert_math(arrived, w_gate, w_up, down_pieces)
    returned = send_home(shares)
    combined = jnp.dot(
        weight_rows, returned.reshape(slot_count, col_share).astype(jnp.float32), precision=highest
    )
    return (resid_cols + combined).astype(jnp.bfloat16)


def solution(mesh):
    in_specs = (
        P("req", None),
        P(),
        P(None, "tp"),
        P(None, "tp"),
        P(),
        P(None, "tp"),
        P(None, "tp"),
        P("tp", None),
        P(),
        P("req", None, "tp"),
        P("req", None, "tp"),
        P("req", "tp", None),
        P("req", None, None),
        P("req", None),
        P("req"),
        P("req", None, None),
        P("req", None),
        P("req", None),
    )
    out_specs = P("req", "tp")
    return jax.shard_map(local, mesh=mesh, in_specs=in_specs, out_specs=out_specs, check_vma=False)
```

```python
import jax
import jax.numpy as jnp
from jax import lax
from jax.sharding import PartitionSpec as P

D = 2048
NOPE = 128
ROPE = 64
VDIM = 128
LATENT = 512
TOPK = 6
EXP_DEV = 1
BEAMS = 8
STEPS = 4
PAGE = 64
PAGES = 8


eps = 1e-06
rope_base = 50000.0


def rms_scale(values):
    return lax.rsqrt(jnp.mean(values * values, axis=-1, keepdims=True) + eps)


def rotate(values, cos_val, sin_val):
    half_rope = values.shape[-1] // 2
    first = values[..., :half_rope]
    second = values[..., half_rope:]
    return jnp.concatenate(
        [first * cos_val - second * sin_val, second * cos_val + first * sin_val], axis=-1
    )


def expert_math(arrived, gate_w, up_w, down_pieces):
    gate_val = jnp.einsum("nesd,edf->nesf", arrived, gate_w, preferred_element_type=jnp.float32)
    up_val = jnp.einsum("nesd,edf->nesf", arrived, up_w, preferred_element_type=jnp.float32)
    active = (jax.nn.silu(gate_val) * up_val).astype(jnp.bfloat16)
    total = None
    for shift, source in enumerate(tp_shifted(active)):
        term = jnp.einsum(
            "nesf,efd->nesd", source, down_pieces[shift], preferred_element_type=jnp.float32
        )
        total = term if total is None else total + term
    return total.astype(jnp.bfloat16)


def tp_shifted(values):
    tp_count = lax.axis_size("tp")
    pieces = [values]
    for shift in range(1, tp_count):
        pieces.append(
            lax.ppermute(values, "tp", [(s, (s + shift) % tp_count) for s in range(tp_count)])
        )
    return pieces


def by_columns(down_w, out_w):
    tp_count = lax.axis_size("tp")
    tp_index = lax.axis_index("tp")
    col_share = out_w.shape[-1] // tp_count
    down_rows = down_w.shape[1]
    down_pieces, out_pieces = [], []
    for shift in range(tp_count):
        start = ((tp_index + shift) % tp_count) * col_share
        piece = jnp.concatenate(
            [
                lax.dynamic_slice_in_dim(down_w[0], start, col_share, 1),
                lax.dynamic_slice_in_dim(out_w, start, col_share, 1),
            ],
            axis=0,
        )
        if shift:
            piece = lax.ppermute(
                piece, "tp", [(s, (s + shift) % tp_count) for s in range(tp_count)]
            )
        down_pieces.append(piece[None, :down_rows])
        out_pieces.append(piece[down_rows:])
    return down_pieces, out_pieces


def send_home(shares):
    return lax.all_to_all(shares, "req", split_axis=0, concat_axis=0, tiled=True)


def local(
    hidden_in,
    attn_gain,
    w_query,
    w_latent,
    kv_gain,
    w_key_up,
    w_value_up,
    w_out,
    moe_gain,
    w_gate,
    w_up,
    w_down,
    latent_cache,
    page_table,
    cache_len,
    parents,
    routes,
    route_weights,
):
    highest = lax.Precision.HIGHEST
    row_count = hidden_in.shape[0]
    req_local = cache_len.shape[0]
    heads_local = w_value_up.shape[1] // VDIM
    tp_count = lax.axis_size("tp")
    req_count = lax.axis_size("req")
    col_share = D // tp_count
    max_len = PAGES * PAGE
    hidden_f = hidden_in.astype(jnp.float32)
    normed = (hidden_f * rms_scale(hidden_f) * attn_gain).astype(jnp.bfloat16)
    normed, down_late, out_late = lax.optimization_barrier((normed, w_down, w_out))
    positions = (
        cache_len.astype(jnp.float32)[:, None, None]
        + jnp.arange(STEPS, dtype=jnp.float32)[None, :, None]
        + jnp.zeros((1, 1, BEAMS), jnp.float32)
    ).reshape(row_count)
    frequency = rope_base ** (-2.0 * jnp.arange(ROPE // 2, dtype=jnp.float32) / ROPE)
    angles = positions[:, None] * frequency[None, :]
    cos_val = jnp.cos(angles)
    sin_val = jnp.sin(angles)
    queries = jnp.dot(normed, w_query, preferred_element_type=jnp.float32).reshape(
        row_count, heads_local, NOPE + ROPE
    )
    q_nope = queries[:, :, :NOPE].astype(jnp.bfloat16)
    q_rope = rotate(queries[:, :, NOPE:], cos_val[:, None, :], sin_val[:, None, :]).astype(
        jnp.bfloat16
    )
    kv_part = jnp.dot(normed, w_latent, preferred_element_type=jnp.float32)
    kv_pieces = tp_shifted(kv_part)[::-1]
    kv_all = lax.dynamic_slice_in_dim(
        jnp.concatenate(kv_pieces + kv_pieces, axis=1),
        (tp_count - 1 - lax.axis_index("tp")) * kv_part.shape[1],
        tp_count * kv_part.shape[1],
        1,
    )
    new_lat = kv_all[:, :LATENT] * rms_scale(kv_all[:, :LATENT]) * kv_gain
    new_rope = rotate(kv_all[:, LATENT:], cos_val, sin_val)
    new_keys = jnp.concatenate([new_lat, new_rope], axis=1).astype(jnp.bfloat16)
    key_up = w_key_up.reshape(LATENT, heads_local, NOPE)
    q_lat = jnp.einsum("nhc,lhc->nhl", q_nope, key_up, preferred_element_type=jnp.float32).astype(
        jnp.bfloat16
    )
    query_key = jnp.concatenate([q_lat, q_rope], axis=2)
    cache_keys = latent_cache.reshape(req_local, max_len, LATENT + ROPE)
    page_hot = page_table[:, :, None] == jnp.arange(PAGES, dtype=jnp.int32)[None, None, :]
    logical_page = jnp.sum(
        jnp.where(page_hot, jnp.arange(PAGES, dtype=jnp.int32)[None, :, None], 0), axis=1
    )
    logical_pos = (
        logical_page[:, :, None] * PAGE + jnp.arange(PAGE, dtype=jnp.int32)[None, None, :]
    ).reshape(req_local, max_len)
    live_mask = logical_pos < cache_len[:, None]
    score_scale = (NOPE + ROPE) ** (-0.5)
    grouped = query_key.reshape(req_local, STEPS * BEAMS * heads_local, LATENT + ROPE)
    s_cache = (
        jnp.einsum("rqd,rld->rql", grouped, cache_keys, preferred_element_type=jnp.float32)
        * score_scale
    )
    s_cache = jnp.where(live_mask[:, None, :], s_cache, -jnp.inf).reshape(
        req_local, STEPS, BEAMS, heads_local, max_len
    )
    fresh = new_keys.reshape(req_local, STEPS, BEAMS, LATENT + ROPE)
    beam_ids = jnp.arange(BEAMS, dtype=jnp.int32)
    lineage_rows = []
    for step_index in range(STEPS):
        lineage = jnp.broadcast_to(beam_ids[None, :], (req_local, BEAMS))
        pieces = [None] * STEPS
        for earlier in range(step_index, -1, -1):
            pieces[earlier] = lineage
            if earlier > 0:
                lineage_hot = lineage[:, :, None] == beam_ids[None, None, :]
                lineage = jnp.sum(
                    jnp.where(lineage_hot, parents[:, earlier - 1][:, None, :], 0), axis=2
                )
        for later in range(step_index + 1, STEPS):
            pieces[later] = jnp.full((req_local, BEAMS), -1, jnp.int32)
        lineage_rows.append(jnp.stack(pieces, axis=2))
    lineage_all = jnp.stack(lineage_rows, axis=1)
    pick = (lineage_all[..., None] == beam_ids).astype(jnp.bfloat16)
    tail_keys = jnp.einsum(
        "rsbja,rjad->rsbjd", pick, fresh, preferred_element_type=jnp.float32
    ).astype(jnp.bfloat16)
    queries_tail = query_key.reshape(req_local, STEPS, BEAMS, heads_local, LATENT + ROPE)
    s_tail = (
        jnp.einsum(
            "rsbhd,rsbjd->rsbhj", queries_tail, tail_keys, preferred_element_type=jnp.float32
        )
        * score_scale
    )
    causal = jnp.arange(STEPS)[None, :] <= jnp.arange(STEPS)[:, None]
    s_tail = jnp.where(causal[None, :, None, None, :], s_tail, -jnp.inf)
    top_score = jnp.maximum(jnp.max(s_cache, axis=-1), jnp.max(s_tail, axis=-1))
    e_cache = jnp.exp(s_cache - top_score[..., None])
    e_tail = jnp.exp(s_tail - top_score[..., None])
    total = jnp.sum(e_cache, axis=-1) + jnp.sum(e_tail, axis=-1)
    p_cache = (e_cache / total[..., None]).astype(jnp.bfloat16)
    p_tail = (e_tail / total[..., None]).astype(jnp.bfloat16)
    context = jnp.einsum(
        "rsbhl,rld->rsbhd", p_cache, cache_keys[..., :LATENT], preferred_element_type=jnp.float32
    )
    context = context + jnp.einsum(
        "rsbhj,rsbjd->rsbhd", p_tail, tail_keys[..., :LATENT], preferred_element_type=jnp.float32
    )
    context = context.astype(jnp.bfloat16).reshape(row_count, heads_local, LATENT)
    value_up = w_value_up.reshape(LATENT, heads_local, VDIM)
    head_out = (
        jnp.einsum("nhl,lhv->nhv", context, value_up, preferred_element_type=jnp.float32)
        .astype(jnp.bfloat16)
        .reshape(row_count, heads_local * VDIM)
    )
    expert_count = EXP_DEV * req_count
    capacity = min(row_count, 2 * row_count * TOPK // expert_count)
    slot_count = expert_count * capacity
    picks = routes.reshape(-1)
    pick_hot = (picks[:, None] == jnp.arange(expert_count, dtype=jnp.int32)[None, :]).astype(
        jnp.int32
    )
    before = jnp.cumsum(pick_hot, axis=0) - pick_hot
    ranks = jnp.sum(before * pick_hot, axis=1)
    slot_of = picks * capacity + ranks
    slot_hot = (slot_of[:, None] == jnp.arange(slot_count, dtype=jnp.int32)[None, :]).reshape(
        row_count, TOPK, slot_count
    )
    gather_rows = jnp.sum(slot_hot.astype(jnp.int32), axis=1).astype(jnp.bfloat16)
    weight_rows = jnp.sum(jnp.where(slot_hot, route_weights[:, :, None], 0.0), axis=1)
    tp_index = lax.axis_index("tp")
    col_start = tp_index * col_share
    head_shift = jnp.concatenate(tp_shifted(head_out), axis=1)
    head_shift, down_pieces, out_pieces = lax.optimization_barrier(
        (head_shift,) + by_columns(down_late, out_late)
    )
    attn_cols = jnp.dot(
        head_shift, jnp.concatenate(out_pieces, axis=0), preferred_element_type=jnp.float32
    )
    hidden_cols = lax.dynamic_slice_in_dim(hidden_f, col_start, col_share, 1)
    resid_cols = hidden_cols + attn_cols
    square_sum = sum(tp_shifted(jnp.sum(resid_cols * resid_cols, axis=-1, keepdims=True)))
    moe_scale = lax.rsqrt(square_sum / D + eps)
    gain_cols = lax.dynamic_slice_in_dim(moe_gain, col_start, col_share, 0)
    moe_in_cols = (resid_cols * moe_scale * gain_cols).astype(jnp.bfloat16)
    placed = jnp.dot(gather_rows.T, moe_in_cols, preferred_element_type=jnp.float32).astype(
        jnp.bfloat16
    )
    arrived_cols = lax.all_to_all(
        placed.reshape(req_count, EXP_DEV, capacity, col_share),
        "req",
        split_axis=0,
        concat_axis=0,
        tiled=True,
    )
    arrived = lax.all_gather(arrived_cols, "tp", axis=3, tiled=True)
    shares = expert_math(arrived, w_gate, w_up, down_pieces)
    returned = send_home(shares)
    combined = jnp.dot(
        weight_rows, returned.reshape(slot_count, col_share).astype(jnp.float32), precision=highest
    )
    return (resid_cols + combined).astype(jnp.bfloat16)


def solution(mesh):
    in_specs = (
        P("req", None),
        P(),
        P(None, "tp"),
        P(None, "tp"),
        P(),
        P(None, "tp"),
        P(None, "tp"),
        P("tp", None),
        P(),
        P("req", None, "tp"),
        P("req", None, "tp"),
        P("req", "tp", None),
        P("req", None, None),
        P("req", None),
        P("req"),
        P("req", None, None),
        P("req", None),
        P("req", None),
    )
    out_specs = P("req", "tp")
    return jax.shard_map(local, mesh=mesh, in_specs=in_specs, out_specs=out_specs, check_vma=False)
```

```python
import jax
import jax.numpy as jnp
from jax import lax
from jax.sharding import PartitionSpec as P

D = 2048
NOPE = 128
ROPE = 64
VDIM = 128
LATENT = 512
TOPK = 6
EXP_DEV = 1
BEAMS = 8
STEPS = 4
PAGE = 64
PAGES = 8


eps = 1e-06
rope_base = 50000.0


def rms_scale(values):
    return lax.rsqrt(jnp.mean(values * values, axis=-1, keepdims=True) + eps)


def rotate(values, cos_val, sin_val):
    half_rope = values.shape[-1] // 2
    first = values[..., :half_rope]
    second = values[..., half_rope:]
    return jnp.concatenate(
        [first * cos_val - second * sin_val, second * cos_val + first * sin_val], axis=-1
    )


def expert_math(arrived_cols, gate_w, up_w, down_pieces):
    tp_count = lax.axis_size("tp")
    tp_index = lax.axis_index("tp")
    col_share = arrived_cols.shape[3]
    gate_val = None
    up_val = None
    for shift, block in enumerate(tp_shifted(arrived_cols)):
        row_start = ((tp_index - shift) % tp_count) * col_share
        gate_term = jnp.einsum(
            "nesd,edf->nesf",
            block,
            lax.dynamic_slice_in_dim(gate_w, row_start, col_share, 1),
            preferred_element_type=jnp.float32,
        )
        up_term = jnp.einsum(
            "nesd,edf->nesf",
            block,
            lax.dynamic_slice_in_dim(up_w, row_start, col_share, 1),
            preferred_element_type=jnp.float32,
        )
        gate_val = gate_term if gate_val is None else gate_val + gate_term
        up_val = up_term if up_val is None else up_val + up_term
    active = (jax.nn.silu(gate_val) * up_val).astype(jnp.bfloat16)
    total = None
    for shift, source in enumerate(tp_shifted(active)):
        term = jnp.einsum(
            "nesf,efd->nesd", source, down_pieces[shift], preferred_element_type=jnp.float32
        )
        total = term if total is None else total + term
    return total.astype(jnp.bfloat16)


def tp_shifted(values):
    tp_count = lax.axis_size("tp")
    pieces = [values]
    for shift in range(1, tp_count):
        pieces.append(
            lax.ppermute(values, "tp", [(s, (s + shift) % tp_count) for s in range(tp_count)])
        )
    return pieces


def by_columns(down_w, out_w):
    tp_count = lax.axis_size("tp")
    tp_index = lax.axis_index("tp")
    col_share = out_w.shape[-1] // tp_count
    down_rows = down_w.shape[1]
    down_pieces, out_pieces = [], []
    for shift in range(tp_count):
        start = ((tp_index + shift) % tp_count) * col_share
        piece = jnp.concatenate(
            [
                lax.dynamic_slice_in_dim(down_w[0], start, col_share, 1),
                lax.dynamic_slice_in_dim(out_w, start, col_share, 1),
            ],
            axis=0,
        )
        if shift:
            piece = lax.ppermute(
                piece, "tp", [(s, (s + shift) % tp_count) for s in range(tp_count)]
            )
        down_pieces.append(piece[None, :down_rows])
        out_pieces.append(piece[down_rows:])
    return down_pieces, out_pieces


def send_home(shares):
    return lax.all_to_all(shares, "req", split_axis=0, concat_axis=0, tiled=True)


def local(
    hidden_in,
    attn_gain,
    w_query,
    w_latent,
    kv_gain,
    w_key_up,
    w_value_up,
    w_out,
    moe_gain,
    w_gate,
    w_up,
    w_down,
    latent_cache,
    page_table,
    cache_len,
    parents,
    routes,
    route_weights,
):
    highest = lax.Precision.HIGHEST
    row_count = hidden_in.shape[0]
    req_local = cache_len.shape[0]
    heads_local = w_value_up.shape[1] // VDIM
    tp_count = lax.axis_size("tp")
    req_count = lax.axis_size("req")
    col_share = D // tp_count
    max_len = PAGES * PAGE
    hidden_f = hidden_in.astype(jnp.float32)
    normed = (hidden_f * rms_scale(hidden_f) * attn_gain).astype(jnp.bfloat16)
    normed, down_late, out_late = lax.optimization_barrier((normed, w_down, w_out))
    positions = (
        cache_len.astype(jnp.float32)[:, None, None]
        + jnp.arange(STEPS, dtype=jnp.float32)[None, :, None]
        + jnp.zeros((1, 1, BEAMS), jnp.float32)
    ).reshape(row_count)
    frequency = rope_base ** (-2.0 * jnp.arange(ROPE // 2, dtype=jnp.float32) / ROPE)
    angles = positions[:, None] * frequency[None, :]
    cos_val = jnp.cos(angles)
    sin_val = jnp.sin(angles)
    queries = jnp.dot(normed, w_query, preferred_element_type=jnp.float32).reshape(
        row_count, heads_local, NOPE + ROPE
    )
    q_nope = queries[:, :, :NOPE].astype(jnp.bfloat16)
    q_rope = rotate(queries[:, :, NOPE:], cos_val[:, None, :], sin_val[:, None, :]).astype(
        jnp.bfloat16
    )
    kv_part = jnp.dot(normed, w_latent, preferred_element_type=jnp.float32)
    kv_pieces = tp_shifted(kv_part)[::-1]
    kv_all = lax.dynamic_slice_in_dim(
        jnp.concatenate(kv_pieces + kv_pieces, axis=1),
        (tp_count - 1 - lax.axis_index("tp")) * kv_part.shape[1],
        tp_count * kv_part.shape[1],
        1,
    )
    new_lat = kv_all[:, :LATENT] * rms_scale(kv_all[:, :LATENT]) * kv_gain
    new_rope = rotate(kv_all[:, LATENT:], cos_val, sin_val)
    new_keys = jnp.concatenate([new_lat, new_rope], axis=1).astype(jnp.bfloat16)
    key_up = w_key_up.reshape(LATENT, heads_local, NOPE)
    q_lat = jnp.einsum("nhc,lhc->nhl", q_nope, key_up, preferred_element_type=jnp.float32).astype(
        jnp.bfloat16
    )
    query_key = jnp.concatenate([q_lat, q_rope], axis=2)
    cache_keys = latent_cache.reshape(req_local, max_len, LATENT + ROPE)
    page_hot = page_table[:, :, None] == jnp.arange(PAGES, dtype=jnp.int32)[None, None, :]
    logical_page = jnp.sum(
        jnp.where(page_hot, jnp.arange(PAGES, dtype=jnp.int32)[None, :, None], 0), axis=1
    )
    logical_pos = (
        logical_page[:, :, None] * PAGE + jnp.arange(PAGE, dtype=jnp.int32)[None, None, :]
    ).reshape(req_local, max_len)
    live_mask = logical_pos < cache_len[:, None]
    score_scale = (NOPE + ROPE) ** (-0.5)
    grouped = query_key.reshape(req_local, STEPS * BEAMS * heads_local, LATENT + ROPE)
    s_cache = (
        jnp.einsum("rqd,rld->rql", grouped, cache_keys, preferred_element_type=jnp.float32)
        * score_scale
    )
    s_cache = jnp.where(live_mask[:, None, :], s_cache, -jnp.inf).reshape(
        req_local, STEPS, BEAMS, heads_local, max_len
    )
    fresh = new_keys.reshape(req_local, STEPS, BEAMS, LATENT + ROPE)
    beam_ids = jnp.arange(BEAMS, dtype=jnp.int32)
    lineage_rows = []
    for step_index in range(STEPS):
        lineage = jnp.broadcast_to(beam_ids[None, :], (req_local, BEAMS))
        pieces = [None] * STEPS
        for earlier in range(step_index, -1, -1):
            pieces[earlier] = lineage
            if earlier > 0:
                lineage_hot = lineage[:, :, None] == beam_ids[None, None, :]
                lineage = jnp.sum(
                    jnp.where(lineage_hot, parents[:, earlier - 1][:, None, :], 0), axis=2
                )
        for later in range(step_index + 1, STEPS):
            pieces[later] = jnp.full((req_local, BEAMS), -1, jnp.int32)
        lineage_rows.append(jnp.stack(pieces, axis=2))
    lineage_all = jnp.stack(lineage_rows, axis=1)
    pick = (lineage_all[..., None] == beam_ids).astype(jnp.bfloat16)
    tail_keys = jnp.einsum(
        "rsbja,rjad->rsbjd", pick, fresh, preferred_element_type=jnp.float32
    ).astype(jnp.bfloat16)
    queries_tail = query_key.reshape(req_local, STEPS, BEAMS, heads_local, LATENT + ROPE)
    s_tail = (
        jnp.einsum(
            "rsbhd,rsbjd->rsbhj", queries_tail, tail_keys, preferred_element_type=jnp.float32
        )
        * score_scale
    )
    causal = jnp.arange(STEPS)[None, :] <= jnp.arange(STEPS)[:, None]
    s_tail = jnp.where(causal[None, :, None, None, :], s_tail, -jnp.inf)
    top_score = jnp.maximum(jnp.max(s_cache, axis=-1), jnp.max(s_tail, axis=-1))
    e_cache = jnp.exp(s_cache - top_score[..., None])
    e_tail = jnp.exp(s_tail - top_score[..., None])
    total = jnp.sum(e_cache, axis=-1) + jnp.sum(e_tail, axis=-1)
    p_cache = (e_cache / total[..., None]).astype(jnp.bfloat16)
    p_tail = (e_tail / total[..., None]).astype(jnp.bfloat16)
    context = jnp.einsum(
        "rsbhl,rld->rsbhd", p_cache, cache_keys[..., :LATENT], preferred_element_type=jnp.float32
    )
    context = context + jnp.einsum(
        "rsbhj,rsbjd->rsbhd", p_tail, tail_keys[..., :LATENT], preferred_element_type=jnp.float32
    )
    context = context.astype(jnp.bfloat16).reshape(row_count, heads_local, LATENT)
    value_up = w_value_up.reshape(LATENT, heads_local, VDIM)
    head_out = (
        jnp.einsum("nhl,lhv->nhv", context, value_up, preferred_element_type=jnp.float32)
        .astype(jnp.bfloat16)
        .reshape(row_count, heads_local * VDIM)
    )
    expert_count = EXP_DEV * req_count
    capacity = min(row_count, 2 * row_count * TOPK // expert_count)
    slot_count = expert_count * capacity
    picks = routes.reshape(-1)
    pick_hot = (picks[:, None] == jnp.arange(expert_count, dtype=jnp.int32)[None, :]).astype(
        jnp.int32
    )
    before = jnp.cumsum(pick_hot, axis=0) - pick_hot
    ranks = jnp.sum(before * pick_hot, axis=1)
    slot_of = picks * capacity + ranks
    slot_hot = (slot_of[:, None] == jnp.arange(slot_count, dtype=jnp.int32)[None, :]).reshape(
        row_count, TOPK, slot_count
    )
    gather_rows = jnp.sum(slot_hot.astype(jnp.int32), axis=1).astype(jnp.bfloat16)
    weight_rows = jnp.sum(jnp.where(slot_hot, route_weights[:, :, None], 0.0), axis=1)
    tp_index = lax.axis_index("tp")
    col_start = tp_index * col_share
    head_shift = jnp.concatenate(tp_shifted(head_out), axis=1)
    head_shift, down_pieces, out_pieces = lax.optimization_barrier(
        (head_shift,) + by_columns(down_late, out_late)
    )
    attn_cols = jnp.dot(
        head_shift, jnp.concatenate(out_pieces, axis=0), preferred_element_type=jnp.float32
    )
    hidden_cols = lax.dynamic_slice_in_dim(hidden_f, col_start, col_share, 1)
    resid_cols = hidden_cols + attn_cols
    square_sum = sum(tp_shifted(jnp.sum(resid_cols * resid_cols, axis=-1, keepdims=True)))
    moe_scale = lax.rsqrt(square_sum / D + eps)
    gain_cols = lax.dynamic_slice_in_dim(moe_gain, col_start, col_share, 0)
    moe_in_cols = (resid_cols * moe_scale * gain_cols).astype(jnp.bfloat16)
    placed = jnp.dot(gather_rows.T, moe_in_cols, preferred_element_type=jnp.float32).astype(
        jnp.bfloat16
    )
    arrived_cols = lax.all_to_all(
        placed.reshape(req_count, EXP_DEV, capacity, col_share),
        "req",
        split_axis=0,
        concat_axis=0,
        tiled=True,
    )
    shares = expert_math(arrived_cols, w_gate, w_up, down_pieces)
    returned = send_home(shares)
    combined = jnp.dot(
        weight_rows, returned.reshape(slot_count, col_share).astype(jnp.float32), precision=highest
    )
    return (resid_cols + combined).astype(jnp.bfloat16)


def solution(mesh):
    in_specs = (
        P("req", None),
        P(),
        P(None, "tp"),
        P(None, "tp"),
        P(),
        P(None, "tp"),
        P(None, "tp"),
        P("tp", None),
        P(),
        P("req", None, "tp"),
        P("req", None, "tp"),
        P("req", "tp", None),
        P("req", None, None),
        P("req", None),
        P("req"),
        P("req", None, None),
        P("req", None),
        P("req", None),
    )
    out_specs = P("req", "tp")
    return jax.shard_map(local, mesh=mesh, in_specs=in_specs, out_specs=out_specs, check_vma=False)
```

```python
import jax
import jax.numpy as jnp
from jax import lax
from jax.sharding import PartitionSpec as P

D = 2048
NOPE = 128
ROPE = 64
VDIM = 128
LATENT = 512
TOPK = 6
EXP_DEV = 1
BEAMS = 8
STEPS = 4
PAGE = 64
PAGES = 8


eps = 1e-06
rope_base = 50000.0


def rms_scale(values):
    return lax.rsqrt(jnp.mean(values * values, axis=-1, keepdims=True) + eps)


def rotate(values, cos_val, sin_val):
    half_rope = values.shape[-1] // 2
    first = values[..., :half_rope]
    second = values[..., half_rope:]
    return jnp.concatenate(
        [first * cos_val - second * sin_val, second * cos_val + first * sin_val], axis=-1
    )


def expert_math(arrived_cols, gate_w, up_w, down_pieces):
    tp_count = lax.axis_size("tp")
    tp_index = lax.axis_index("tp")
    col_share = arrived_cols.shape[3]
    gate_val = None
    up_val = None
    for shift, block in enumerate(tp_shifted(arrived_cols)):
        row_start = ((tp_index - shift) % tp_count) * col_share
        gate_term = jnp.einsum(
            "nesd,edf->nesf",
            block,
            lax.dynamic_slice_in_dim(gate_w, row_start, col_share, 1),
            preferred_element_type=jnp.float32,
        )
        up_term = jnp.einsum(
            "nesd,edf->nesf",
            block,
            lax.dynamic_slice_in_dim(up_w, row_start, col_share, 1),
            preferred_element_type=jnp.float32,
        )
        gate_val = gate_term if gate_val is None else gate_val + gate_term
        up_val = up_term if up_val is None else up_val + up_term
    active = (jax.nn.silu(gate_val) * up_val).astype(jnp.bfloat16)
    total = None
    for shift, source in enumerate(tp_shifted(active)):
        term = jnp.einsum(
            "nesf,efd->nesd", source, down_pieces[shift], preferred_element_type=jnp.float32
        )
        total = term if total is None else total + term
    return total.astype(jnp.bfloat16)


def tp_shifted(values):
    tp_count = lax.axis_size("tp")
    pieces = [values]
    for shift in range(1, tp_count):
        pieces.append(
            lax.ppermute(values, "tp", [(s, (s + shift) % tp_count) for s in range(tp_count)])
        )
    return pieces


def by_columns(down_w, out_w):
    tp_count = lax.axis_size("tp")
    tp_index = lax.axis_index("tp")
    col_share = out_w.shape[-1] // tp_count
    down_rows = down_w.shape[1]
    down_pieces, out_pieces = [], []
    for shift in range(tp_count):
        start = ((tp_index + shift) % tp_count) * col_share
        piece = jnp.concatenate(
            [
                lax.dynamic_slice_in_dim(down_w[0], start, col_share, 1),
                lax.dynamic_slice_in_dim(out_w, start, col_share, 1),
            ],
            axis=0,
        )
        if shift:
            piece = lax.ppermute(
                piece, "tp", [(s, (s + shift) % tp_count) for s in range(tp_count)]
            )
        down_pieces.append(piece[None, :down_rows])
        out_pieces.append(piece[down_rows:])
    return down_pieces, out_pieces


def send_home(shares):
    return lax.all_to_all(shares, "req", split_axis=0, concat_axis=0, tiled=True)


def local(
    hidden_in,
    attn_gain,
    w_query,
    w_latent,
    kv_gain,
    w_key_up,
    w_value_up,
    w_out,
    moe_gain,
    w_gate,
    w_up,
    w_down,
    latent_cache,
    page_table,
    cache_len,
    parents,
    routes,
    route_weights,
):
    highest = lax.Precision.HIGHEST
    row_count = hidden_in.shape[0]
    req_local = cache_len.shape[0]
    heads_local = w_value_up.shape[1] // VDIM
    tp_count = lax.axis_size("tp")
    req_count = lax.axis_size("req")
    col_share = D // tp_count
    max_len = PAGES * PAGE
    hidden_f = hidden_in.astype(jnp.float32)
    normed = (hidden_f * rms_scale(hidden_f) * attn_gain).astype(jnp.bfloat16)
    normed, down_late, out_late = lax.optimization_barrier((normed, w_down, w_out))
    positions = (
        cache_len.astype(jnp.float32)[:, None, None]
        + jnp.arange(STEPS, dtype=jnp.float32)[None, :, None]
        + jnp.zeros((1, 1, BEAMS), jnp.float32)
    ).reshape(row_count)
    frequency = rope_base ** (-2.0 * jnp.arange(ROPE // 2, dtype=jnp.float32) / ROPE)
    angles = positions[:, None] * frequency[None, :]
    cos_val = jnp.cos(angles)
    sin_val = jnp.sin(angles)
    queries = jnp.dot(normed, w_query, preferred_element_type=jnp.float32).reshape(
        row_count, heads_local, NOPE + ROPE
    )
    q_nope = queries[:, :, :NOPE].astype(jnp.bfloat16)
    q_rope = rotate(queries[:, :, NOPE:], cos_val[:, None, :], sin_val[:, None, :]).astype(
        jnp.bfloat16
    )
    kv_part = jnp.dot(normed, w_latent, preferred_element_type=jnp.float32)
    kv_pieces = tp_shifted(kv_part)[::-1]
    kv_all = lax.dynamic_slice_in_dim(
        jnp.concatenate(kv_pieces + kv_pieces, axis=1),
        (tp_count - 1 - lax.axis_index("tp")) * kv_part.shape[1],
        tp_count * kv_part.shape[1],
        1,
    )
    new_lat = kv_all[:, :LATENT] * rms_scale(kv_all[:, :LATENT]) * kv_gain
    new_rope = rotate(kv_all[:, LATENT:], cos_val, sin_val)
    new_keys = jnp.concatenate([new_lat, new_rope], axis=1).astype(jnp.bfloat16)
    key_up = w_key_up.reshape(LATENT, heads_local, NOPE)
    q_lat = jnp.einsum("nhc,lhc->nhl", q_nope, key_up, preferred_element_type=jnp.float32).astype(
        jnp.bfloat16
    )
    query_key = jnp.concatenate([q_lat, q_rope], axis=2)
    cache_keys = latent_cache.reshape(req_local, max_len, LATENT + ROPE)
    page_hot = page_table[:, :, None] == jnp.arange(PAGES, dtype=jnp.int32)[None, None, :]
    logical_page = jnp.sum(
        jnp.where(page_hot, jnp.arange(PAGES, dtype=jnp.int32)[None, :, None], 0), axis=1
    )
    logical_pos = (
        logical_page[:, :, None] * PAGE + jnp.arange(PAGE, dtype=jnp.int32)[None, None, :]
    ).reshape(req_local, max_len)
    live_mask = logical_pos < cache_len[:, None]
    score_scale = (NOPE + ROPE) ** (-0.5)
    grouped = query_key.reshape(req_local, STEPS * BEAMS * heads_local, LATENT + ROPE)
    s_cache = (
        jnp.einsum("rqd,rld->rql", grouped, cache_keys, preferred_element_type=jnp.float32)
        * score_scale
    )
    s_cache = jnp.where(live_mask[:, None, :], s_cache, -jnp.inf).reshape(
        req_local, STEPS, BEAMS, heads_local, max_len
    )
    fresh = new_keys.reshape(req_local, STEPS, BEAMS, LATENT + ROPE)
    beam_ids = jnp.arange(BEAMS, dtype=jnp.int32)
    lineage_rows = []
    for step_index in range(STEPS):
        lineage = jnp.broadcast_to(beam_ids[None, :], (req_local, BEAMS))
        pieces = [None] * STEPS
        for earlier in range(step_index, -1, -1):
            pieces[earlier] = lineage
            if earlier > 0:
                lineage_hot = lineage[:, :, None] == beam_ids[None, None, :]
                lineage = jnp.sum(
                    jnp.where(lineage_hot, parents[:, earlier - 1][:, None, :], 0), axis=2
                )
        for later in range(step_index + 1, STEPS):
            pieces[later] = jnp.full((req_local, BEAMS), -1, jnp.int32)
        lineage_rows.append(jnp.stack(pieces, axis=2))
    lineage_all = jnp.stack(lineage_rows, axis=1)
    pick = (lineage_all[..., None] == beam_ids).astype(jnp.bfloat16)
    tail_keys = jnp.einsum(
        "rsbja,rjad->rsbjd", pick, fresh, preferred_element_type=jnp.float32
    ).astype(jnp.bfloat16)
    queries_tail = query_key.reshape(req_local, STEPS, BEAMS, heads_local, LATENT + ROPE)
    s_tail = (
        jnp.einsum(
            "rsbhd,rsbjd->rsbhj", queries_tail, tail_keys, preferred_element_type=jnp.float32
        )
        * score_scale
    )
    causal = jnp.arange(STEPS)[None, :] <= jnp.arange(STEPS)[:, None]
    s_tail = jnp.where(causal[None, :, None, None, :], s_tail, -jnp.inf)
    top_score = jnp.maximum(jnp.max(s_cache, axis=-1), jnp.max(s_tail, axis=-1))
    e_cache = jnp.exp(s_cache - top_score[..., None])
    e_tail = jnp.exp(s_tail - top_score[..., None])
    total = jnp.sum(e_cache, axis=-1) + jnp.sum(e_tail, axis=-1)
    p_cache = (e_cache / total[..., None]).astype(jnp.bfloat16)
    p_tail = (e_tail / total[..., None]).astype(jnp.bfloat16)
    context = jnp.einsum(
        "rsbhl,rld->rsbhd", p_cache, cache_keys[..., :LATENT], preferred_element_type=jnp.float32
    )
    context = context + jnp.einsum(
        "rsbhj,rsbjd->rsbhd", p_tail, tail_keys[..., :LATENT], preferred_element_type=jnp.float32
    )
    context = context.astype(jnp.bfloat16).reshape(row_count, heads_local, LATENT)
    value_up = w_value_up.reshape(LATENT, heads_local, VDIM)
    head_out = (
        jnp.einsum("nhl,lhv->nhv", context, value_up, preferred_element_type=jnp.float32)
        .astype(jnp.bfloat16)
        .reshape(row_count, heads_local * VDIM)
    )
    expert_count = EXP_DEV * req_count
    capacity = min(row_count, 2 * row_count * TOPK // expert_count)
    slot_count = expert_count * capacity
    picks = routes.reshape(-1)
    pick_hot = (picks[:, None] == jnp.arange(expert_count, dtype=jnp.int32)[None, :]).astype(
        jnp.int32
    )
    before = jnp.cumsum(pick_hot, axis=0) - pick_hot
    ranks = jnp.sum(before * pick_hot, axis=1)
    slot_of = picks * capacity + ranks
    slot_hot = (slot_of[:, None] == jnp.arange(slot_count, dtype=jnp.int32)[None, :]).reshape(
        row_count, TOPK, slot_count
    )
    gather_rows = jnp.sum(slot_hot.astype(jnp.int32), axis=1).astype(jnp.bfloat16)
    weight_rows = jnp.sum(jnp.where(slot_hot, route_weights[:, :, None], 0.0), axis=1)
    tp_index = lax.axis_index("tp")
    col_start = tp_index * col_share
    head_shift = jnp.concatenate(tp_shifted(head_out), axis=1)
    head_shift, down_pieces, out_pieces = lax.optimization_barrier(
        (head_shift,) + by_columns(down_late, out_late)
    )
    attn_cols = jnp.dot(
        head_shift, jnp.concatenate(out_pieces, axis=0), preferred_element_type=jnp.float32
    )
    hidden_cols = lax.dynamic_slice_in_dim(hidden_f, col_start, col_share, 1)
    resid_cols = hidden_cols + attn_cols
    square_sum = sum(tp_shifted(jnp.sum(resid_cols * resid_cols, axis=-1, keepdims=True)))
    moe_scale = lax.rsqrt(square_sum / D + eps)
    gain_cols = lax.dynamic_slice_in_dim(moe_gain, col_start, col_share, 0)
    moe_in_cols = (resid_cols * moe_scale * gain_cols).astype(jnp.bfloat16)
    placed = jnp.dot(gather_rows.T, moe_in_cols, preferred_element_type=jnp.float32).astype(
        jnp.bfloat16
    )
    arrived_cols = lax.all_to_all(
        placed.reshape(req_count, EXP_DEV, capacity, col_share),
        "req",
        split_axis=0,
        concat_axis=0,
        tiled=True,
    )
    shares = expert_math(arrived_cols, w_gate, w_up, down_pieces)
    returned = send_home(shares)
    returned_rows = returned.reshape(slot_count, col_share)
    weight_hi = weight_rows.astype(jnp.bfloat16)
    weight_lo = (weight_rows - weight_hi.astype(jnp.float32)).astype(jnp.bfloat16)
    combined = jnp.dot(weight_hi, returned_rows, preferred_element_type=jnp.float32) + jnp.dot(
        weight_lo, returned_rows, preferred_element_type=jnp.float32
    )
    return (resid_cols + combined).astype(jnp.bfloat16)


def solution(mesh):
    in_specs = (
        P("req", None),
        P(),
        P(None, "tp"),
        P(None, "tp"),
        P(),
        P(None, "tp"),
        P(None, "tp"),
        P("tp", None),
        P(),
        P("req", None, "tp"),
        P("req", None, "tp"),
        P("req", "tp", None),
        P("req", None, None),
        P("req", None),
        P("req"),
        P("req", None, None),
        P("req", None),
        P("req", None),
    )
    out_specs = P("req", "tp")
    return jax.shard_map(local, mesh=mesh, in_specs=in_specs, out_specs=out_specs, check_vma=False)
```
